128 devices in a mesh: table: 4 (over y), blk: 32 (over z, x, core).
Axes of the slice: x: 4, y: 4, z: 4, core: 2. Of those that a mesh axis runs over, the one named last changes fastest.
Arguments:
- residual: bfloat16 [4, 4096, 512], P('table', 'blk'), may hold values from -6 to 6
- queries: bfloat16 [4, 4096, 512], P('table', 'blk'), may hold values from -26 to 26
- key_rows: bfloat16 [4, 4096, 512], P('table', 'blk'), may hold values from -26 to 26
- value_rows: bfloat16 [4, 4096, 512], P('table', 'blk'), may hold values from -6 to 6
- w_out: bfloat16 [512, 512], replicated, may hold values from -0.25 to 0.25
- expert_ids: int32 [4, 4096, 2], P('table', 'blk'), may hold values from 0 to 63, all different within a row; in each aligned block of 128 rows (0 to 127, 128 to 255, ..., all dimensions but the last counted through in order) at most 12 rows name the same one
- route_gates: float32 [4, 4096, 2], P('table', 'blk'), may hold values from 0.2 to 1
- cotangent: bfloat16 [4, 4096, 512], P('table', 'blk'), may hold values from -6 to 6
- w_gate: bfloat16 [128, 512, 1024], P(('table', 'blk')), may hold values from -0.25 to 0.25
- w_up: bfloat16 [128, 512, 1024], P(('table', 'blk')), may hold values from -0.25 to 0.25
- w_down: bfloat16 [128, 1024, 512], P(('table', 'blk')), may hold values from -0.125 to 0.125
Outputs:
- block_out: bfloat16 [4, 4096, 512], P('table', 'blk')
- grad_stream: bfloat16 [4, 4096, 512], P('table', 'blk')
- grad_gate: bfloat16 [128, 512, 1024], P(('table', 'blk'))
- grad_up: bfloat16 [128, 512, 1024], P(('table', 'blk'))
- grad_down: bfloat16 [128, 1024, 512], P(('table', 'blk'))
The draws below stay inside these ranges and needn't reach their ends.
Inputs may be any that keep to these rules, and one draw needn't show every extreme that they name: `expert_ids`: each row names 2 different experts; in the rows of one device (aligned blocks of 128 rows of a table) no expert is named by more than 12 rows, a bound that some block reaches.
All inputs are finite; a program needn't handle non-finite values.
Results may differ from the reference program's by a relative error of at most 0.011.
Values may be sent and summed in bfloat16 or wider, within the bound.
No kernel may reach another device: no remote copies, remote signals or barrier semaphores. Data moves between devices by JAX's collectives and lax.ppermute only.
A program may use at most 128 MiB of HBM per device.

```python
import math
import jax
import jax.numpy as jnp
import numpy as np
from jax import lax

D = 512
HEADS = 8
HEAD = 64
EXPERTS = 64
FF = 2048
TOP = 2
PIECES = 2
ROWS_DEV = 128
TABLES = 4
SEQ = 4096
CAP = 12
FH = 1024
N_TABLE = 4
N_BLK = 32


def attention_pair(key):
    base = jax.random.fold_in(key, 7)
    first_key, second_key = jax.random.split(base, 2)
    drawn_queries = jnp.clip(jax.random.normal(first_key, (TABLES, SEQ, D), jnp.float32), -4.0, 4.0) * 1.6
    drawn_keys = jnp.clip(jax.random.normal(second_key, (TABLES, SEQ, D), jnp.float32), -4.0, 4.0) * 1.6
    query_out = drawn_queries
    key_out = drawn_keys
    return (query_out, key_out)


def draw_queries(key, part):
    return attention_pair(key)[0].astype(jnp.bfloat16)


def draw_key_rows(key, part):
    return attention_pair(key)[1].astype(jnp.bfloat16)


def block_scale(stream_key, shape, pieces, smallest, top_value):
    def one(dim, shards_of):
        heights = jax.random.uniform(jax.random.fold_in(jax.random.fold_in(stream_key, 6), dim), (shards_of,), jnp.float32, smallest / len(pieces), top_value / len(pieces))
        return jnp.repeat(jnp.exp(heights), shape[dim] // shards_of).reshape((-1,) + (1,) * (len(shape) - dim - 1))

    level = one(*pieces[0])
    for cut in pieces[1:]:
        level = level * one(*cut)
    return level


def deal_out(rng, own, number, rows, number_of, top, bound, slope):
    sequence = jax.random.permutation(rng, number_of)
    crowded, usual = portions_of(number_of, rows * top, bound, slope, True), portions_of(number_of, rows * top, bound, slope, False)
    places = jnp.arange(number_of)

    def named(sizes, turn):
        used = int((sizes > 0).sum())
        fixed = max(1, used // 4)
        moved = fixed + (places - fixed + turn * (used - fixed)) % max(1, number_of - fixed)
        return jnp.zeros((number_of,), jnp.int32).at[sequence[jnp.where(places < fixed, places, moved)]].set(jnp.asarray(sizes, jnp.int32))

    sizes = jnp.where(number % 4 == 0, named(crowded, number // 4), named(usual, number - number // 4 - 1))
    mixed = jax.random.permutation(jax.random.fold_in(own, 3), number_of)
    giver, sink = mixed[0:number_of // 2 * 2:2], mixed[1:number_of // 2 * 2:2]
    room = jnp.minimum(sizes[giver] - 1, bound - sizes[sink]) // 2
    room = jnp.where((giver == sequence[0]) | (sink == sequence[0]) | (sizes[sink] == 0), 0, jnp.maximum(room, 0))
    moved = jax.random.randint(jax.random.fold_in(own, 4), (number_of // 2,), 0, 1 << 20) % (room + 1)
    sizes = sizes.at[giver].add(-moved).at[sink].add(moved)
    items = jnp.searchsorted(jnp.cumsum(sizes), jnp.arange(rows * top), side="right").astype(jnp.int32)
    grid = items.reshape(top, rows).T
    grid = grid[jax.random.permutation(jax.random.fold_in(own, 1), rows)]
    turn = jax.random.randint(jax.random.fold_in(own, 2), (rows, 1), 0, top)
    return jnp.take_along_axis(grid, (jnp.arange(top)[None, :] + turn) % top, axis=1)


def portions_of(amount, total, most, lean, full):
    loads = [(1 << 20) // math.isqrt(grade ** lean) + 1 for grade in range(1, amount + 1)]
    largest = most if full else min(most, max(-(-total // amount), total * loads[0] // sum(loads)))
    least = 1 if total - largest >= amount - 1 else 0
    given, rest = [largest] + [least] * (amount - 1), total - largest - least * (amount - 1)
    while rest > 0:
        candidates = [i for i in range(1, amount) if given[i] < largest] or [i for i in range(1, amount) if given[i] < most]
        pool, remaining = sum([loads[i] for i in candidates]), rest
        for i in candidates:
            extra = min(most - given[i], max(1, remaining * loads[i] // pool), rest)
            given[i] = given[i] + extra
            rest = rest - extra
    return np.array(given)


def centred(rng, dims, deviation, reach, cuts=(), held_as=jnp.bfloat16):
    factor_of = block_scale(rng, dims, cuts, -0.22, 0.18) if cuts else 1.0
    values = jax.random.normal(rng, dims, jnp.float32) * deviation * factor_of
    return jnp.minimum(jnp.maximum(values, -reach), reach).astype(held_as)


def setup_inputs(seed: int = 0) -> dict:
    key_of = jax.random.split(jax.random.key(seed), 12)
    residual = centred(key_of[0], (TABLES, SEQ, D), 1.0, 6.0, ((0, 4), (1, 32)))
    queries = draw_queries(jax.random.fold_in(key_of[11], 71), 0)
    key_rows = draw_key_rows(jax.random.fold_in(key_of[11], 71), 0)
    value_rows = centred(key_of[3], (TABLES, SEQ, D), 1.0, 6.0, ((0, 4), (1, 32)))
    w_out = centred(key_of[4], (D, D), D ** -0.5, 0.25)
    expert_ids_keys = jax.random.split(jax.random.fold_in(key_of[5], 1), TABLES * SEQ // ROWS_DEV)
    expert_ids_turns = jax.random.permutation(jax.random.fold_in(key_of[5], 3), TABLES * SEQ // ROWS_DEV)
    expert_ids = jax.vmap(lambda own, number: deal_out(jax.random.fold_in(key_of[5], 2), own, number, ROWS_DEV, EXPERTS, TOP, CAP, 2))(expert_ids_keys, expert_ids_turns).reshape((TABLES, SEQ, TOP))
    route_gates = jnp.clip(jnp.exp(math.log(1.0) - 1.609438 * jax.random.uniform(key_of[6], (TABLES, SEQ, TOP), jnp.float32) ** block_scale(key_of[6], (TABLES, SEQ, TOP), ((0, 4), (1, 32)), -0.2, 0.2)), 0.2, 1.0)
    cotangent = centred(key_of[7], (TABLES, SEQ, D), 1.0, 6.0, ((0, 4), (1, 32)))
    w_gate = centred(key_of[8], (PIECES * EXPERTS, D, FH), D ** -0.5, 0.25, ((0, 128),))
    w_up = centred(key_of[9], (PIECES * EXPERTS, D, FH), D ** -0.5, 0.25, ((0, 128),))
    w_down = centred(key_of[10], (PIECES * EXPERTS, FH, D), FF ** -0.5, 0.125, ((0, 128),))
    return dict(residual=residual, queries=queries, key_rows=key_rows, value_rows=value_rows, w_out=w_out, expert_ids=expert_ids, route_gates=route_gates, cotangent=cotangent, w_gate=w_gate, w_up=w_up, w_down=w_down)


def normalize(stream):
    radius = jnp.sqrt(lax.optimization_barrier(jnp.mean(stream * stream, axis=-1, keepdims=True)) + 1e-06)
    return (stream / radius, radius)

def silu_grad(pre):
    sig = jax.nn.sigmoid(pre)
    return sig * (1.0 + pre * (1.0 - sig))

def attend(trio):
    query_rows, key_table, value_table = trio
    scale = 1.0 / math.sqrt(HEAD)
    key_heads = key_table.astype(jnp.float32).reshape(SEQ, HEADS, HEAD)
    value_heads = value_table.astype(jnp.float32).reshape(SEQ, HEADS, HEAD)
    block = min(512, SEQ)
    grouped = query_rows.astype(jnp.float32).reshape(SEQ // block, block, HEADS, HEAD)

    def one_block(query_block):
        scores = jnp.einsum('qhd,khd->hqk', query_block, key_heads) * scale
        highest = lax.optimization_barrier(jnp.max(scores, axis=-1, keepdims=True))
        expo = jnp.exp(scores - highest)
        denom = lax.optimization_barrier(jnp.sum(expo, axis=-1))
        probs = lax.optimization_barrier(expo.astype(jnp.bfloat16)).astype(jnp.float32)
        totals = jnp.einsum('hqk,khd->hqd', probs, value_heads)
        mixed = totals / denom[..., None]
        return jnp.transpose(mixed, (1, 0, 2)).reshape(block, D).astype(jnp.bfloat16)
    return lax.map(one_block, grouped).reshape(SEQ, D)

def expert_piece(inputs, cots, gate_mat, up_mat, down_mat):
    pre_gate = jnp.dot(inputs, gate_mat, preferred_element_type=jnp.float32)
    pre_up = jnp.dot(inputs, up_mat, preferred_element_type=jnp.float32)
    hidden = (jax.nn.silu(pre_gate) * pre_up).astype(jnp.bfloat16)
    output = jnp.dot(hidden, down_mat, preferred_element_type=jnp.float32).astype(jnp.bfloat16)
    grad_hidden = jnp.dot(cots, down_mat.T, preferred_element_type=jnp.float32)
    grad_pre_gate = (grad_hidden * pre_up * silu_grad(pre_gate)).astype(jnp.bfloat16)
    grad_pre_up = (grad_hidden * jax.nn.silu(pre_gate)).astype(jnp.bfloat16)
    grad_down_mat = jnp.dot(hidden.T, cots, preferred_element_type=jnp.float32)
    grad_gate_mat = jnp.dot(inputs.T, grad_pre_gate, preferred_element_type=jnp.float32)
    grad_up_mat = jnp.dot(inputs.T, grad_pre_up, preferred_element_type=jnp.float32)
    grad_inputs = (jnp.dot(grad_pre_gate, gate_mat.T, preferred_element_type=jnp.float32) + jnp.dot(grad_pre_up, up_mat.T, preferred_element_type=jnp.float32)).astype(jnp.bfloat16)
    return (output, grad_inputs, grad_gate_mat, grad_up_mat, grad_down_mat)

def reference(residual, queries, key_rows, value_rows, w_out, expert_ids, route_gates, cotangent, w_gate, w_up, w_down):
    attended = lax.map(attend, (queries, key_rows, value_rows))
    flat_stream = residual.reshape(-1, D).astype(jnp.float32) + jnp.dot(attended.reshape(-1, D), w_out, preferred_element_type=jnp.float32)
    unit, radius = normalize(flat_stream)
    normed = unit.astype(jnp.bfloat16)
    route_experts = expert_ids.reshape(-1).astype(jnp.int32)
    gates = route_gates.reshape(-1).astype(jnp.float32)
    route_count = route_experts.shape[0]
    source_row = (jnp.arange(route_count, dtype=jnp.int32) // TOP).astype(jnp.int32)
    order = jnp.argsort(route_experts, stable=True).astype(jnp.int32)
    counts = lax.optimization_barrier(jnp.sum((route_experts[:, None] == jnp.arange(EXPERTS, dtype=jnp.int32)[None, :]).astype(jnp.int32), axis=0))
    offsets = (jnp.cumsum(counts) - counts).astype(jnp.int32)
    capacity = N_TABLE * N_BLK * CAP
    padded = jnp.concatenate([order, jnp.zeros((capacity,), jnp.int32)])
    grad_flat = cotangent.reshape(-1, D).astype(jnp.float32)

    def per_expert(expert):
        picked = lax.dynamic_slice(padded, (offsets[expert].astype(jnp.int32),), (capacity,))
        live = jnp.arange(capacity, dtype=jnp.int32) < counts[expert]
        rows = source_row[picked]
        inputs = jnp.where(live[:, None], normed[rows], jnp.zeros((), jnp.bfloat16))
        cots = jnp.where(live[:, None], (gates[picked][:, None] * grad_flat[rows]).astype(jnp.bfloat16), jnp.zeros((), jnp.bfloat16))
        combined = jnp.zeros((capacity, D), jnp.float32)
        grads_in = jnp.zeros((capacity, D), jnp.float32)
        gate_list, up_list, down_list = ([], [], [])
        for piece in range(PIECES):
            index = expert * PIECES + piece
            output, grad_inputs, grad_gate_mat, grad_up_mat, grad_down_mat = expert_piece(inputs, cots, w_gate[index], w_up[index], w_down[index])
            combined = combined + output.astype(jnp.float32)
            grads_in = grads_in + grad_inputs.astype(jnp.float32)
            gate_list.append(grad_gate_mat)
            up_list.append(grad_up_mat)
            down_list.append(grad_down_mat)
        target = jnp.where(live, picked, route_count).astype(jnp.int32)
        return (combined, grads_in, target, jnp.stack(gate_list), jnp.stack(up_list), jnp.stack(down_list))
    combined, grads_in, target, gate_grads, up_grads, down_grads = lax.map(per_expert, jnp.arange(EXPERTS, dtype=jnp.int32))
    flat_target = target.reshape(-1)
    route_out = jnp.zeros((route_count + 1, D), jnp.float32).at[flat_target].add(combined.reshape(-1, D))[:route_count]
    route_grad = jnp.zeros((route_count + 1, D), jnp.float32).at[flat_target].add(grads_in.reshape(-1, D))[:route_count]
    moe = lax.optimization_barrier(jnp.sum((gates[:, None] * route_out).reshape(-1, TOP, D), axis=1))
    block_out = (flat_stream + moe).astype(jnp.bfloat16).reshape(residual.shape)
    grad_unit = lax.optimization_barrier(jnp.sum(route_grad.reshape(-1, TOP, D), axis=1))
    grad_stream = grad_flat + (grad_unit - unit * lax.optimization_barrier(jnp.mean(grad_unit * unit, axis=-1, keepdims=True))) / radius
    grad_stream = grad_stream.astype(jnp.bfloat16).reshape(residual.shape)
    grad_gate = gate_grads.reshape(PIECES * EXPERTS, D, FH).astype(jnp.bfloat16)
    grad_up = up_grads.reshape(PIECES * EXPERTS, D, FH).astype(jnp.bfloat16)
    grad_down = down_grads.reshape(PIECES * EXPERTS, FH, D).astype(jnp.bfloat16)
    return (block_out, grad_stream, grad_gate, grad_up, grad_down)
```

```python
import math

import jax
import jax.numpy as jnp
from jax import lax
from jax.sharding import PartitionSpec as P

D = 512
HEADS = 8
HEAD = 64
EXPERTS = 64
TOP = 2
PIECES = 2
CAP = 12


def silu_grad(pre):
    sig = jax.nn.sigmoid(pre)
    return sig * (1.0 + pre * (1.0 - sig))


def to_experts(buffer):
    return lax.all_to_all(buffer, ("table", "blk"), split_axis=0, concat_axis=0, tiled=True)


def to_anchor(buffer):
    return lax.all_to_all(buffer, ("table", "blk"), split_axis=0, concat_axis=0, tiled=True)


def forward_part(arrived, w_gate, w_up, w_down):
    pre_gate = jnp.einsum("svcd,vdf->svcf", arrived, w_gate, preferred_element_type=jnp.float32)
    pre_up = jnp.einsum("svcd,vdf->svcf", arrived, w_up, preferred_element_type=jnp.float32)
    activated = jax.nn.silu(pre_gate)
    hidden = (activated * pre_up).astype(jnp.bfloat16)
    outputs = jnp.einsum(
        "svcf,vfd->svcd", hidden, w_down, preferred_element_type=jnp.float32
    ).astype(jnp.bfloat16)
    return (outputs, pre_gate, pre_up, activated, hidden)


def backward_part(arrived, arrived_cots, pre_gate, pre_up, activated, hidden, w_gate, w_up, w_down):
    grad_hidden = jnp.einsum(
        "svcd,vfd->svcf", arrived_cots, w_down, preferred_element_type=jnp.float32
    )
    grad_pre_gate = (grad_hidden * pre_up * silu_grad(pre_gate)).astype(jnp.bfloat16)
    grad_pre_up = (grad_hidden * activated).astype(jnp.bfloat16)
    grad_down = jnp.einsum(
        "svcf,svcd->vfd", hidden, arrived_cots, preferred_element_type=jnp.float32
    ).astype(jnp.bfloat16)
    grad_gate = jnp.einsum(
        "svcd,svcf->vdf", arrived, grad_pre_gate, preferred_element_type=jnp.float32
    ).astype(jnp.bfloat16)
    grad_up = jnp.einsum(
        "svcd,svcf->vdf", arrived, grad_pre_up, preferred_element_type=jnp.float32
    ).astype(jnp.bfloat16)
    grad_inputs = (
        jnp.einsum("svcf,vdf->svcd", grad_pre_gate, w_gate, preferred_element_type=jnp.float32)
        + jnp.einsum("svcf,vdf->svcd", grad_pre_up, w_up, preferred_element_type=jnp.float32)
    ).astype(jnp.bfloat16)
    return (grad_inputs, grad_gate, grad_up, grad_down)


def attend_heads(query_rows, key_rows, value_rows):
    rows = query_rows.shape[0]
    devices = lax.psum(1, "blk")
    groups = devices // HEADS
    part = rows // groups
    scale = 1.0 / math.sqrt(HEAD)

    def by_head(block):
        heads = jnp.transpose(block.reshape(rows, HEADS, HEAD), (1, 0, 2))
        return jnp.broadcast_to(heads[:, None], (HEADS, groups, rows, HEAD)).reshape(devices, rows, HEAD)

    pairs = jnp.concatenate([by_head(key_rows), by_head(value_rows)], axis=-1)
    asked = jnp.transpose(query_rows.reshape(groups, part, HEADS, HEAD), (2, 0, 1, 3))
    asked = asked.reshape(devices, part, HEAD)
    asked = jnp.concatenate([asked, jnp.zeros_like(asked)], axis=-1)
    parcel = jnp.concatenate([pairs, asked], axis=1)
    got = lax.all_to_all(parcel, "blk", 0, 0, tiled=True)
    keys = got[:, :rows, :HEAD].reshape(devices * rows, HEAD)
    values = got[:, :rows, HEAD:].reshape(devices * rows, HEAD)
    mine = got[:, rows:, :HEAD].reshape(devices * part, HEAD)
    scores = jnp.dot(mine, keys.T, preferred_element_type=jnp.float32) * scale
    highest = jnp.max(scores, axis=-1, keepdims=True)
    expo = jnp.exp(scores - highest)
    denom = jnp.sum(expo, axis=-1, keepdims=True)
    totals = jnp.dot(expo.astype(jnp.bfloat16), values, preferred_element_type=jnp.float32)
    mixed = (totals / denom).astype(jnp.bfloat16).reshape(devices, part, HEAD)
    back = lax.all_to_all(mixed, "blk", 0, 0, tiled=True)
    back = jnp.transpose(back.reshape(HEADS, groups, part, HEAD), (1, 2, 0, 3))
    return back.reshape(rows, HEADS * HEAD)


def body(
    residual,
    queries,
    key_rows,
    value_rows,
    w_out,
    expert_ids,
    route_gates,
    cotangent,
    w_gate,
    w_up,
    w_down,
):
    row_count = queries.shape[1]
    attended = attend_heads(queries[0], key_rows[0], value_rows[0])
    stream = residual[0].astype(jnp.float32) + jnp.dot(
        attended, w_out, preferred_element_type=jnp.float32
    )
    radius = jnp.sqrt(jnp.mean(stream * stream, axis=-1, keepdims=True) + 1e-06)
    unit = stream / radius
    normed = unit.astype(jnp.bfloat16)
    route_experts = expert_ids[0].reshape(-1)
    gates = route_gates[0].reshape(-1)
    onehot = (route_experts[:, None] == jnp.arange(EXPERTS, dtype=jnp.int32)[None, :]).astype(
        jnp.int32
    )
    before = jnp.cumsum(onehot, axis=0) - onehot
    position = jnp.sum(before * onehot, axis=1)
    slot_index = route_experts * CAP + position
    local_pieces = w_gate.shape[0]
    senders = PIECES * EXPERTS // local_pieces

    def collect(returned):
        summed = jnp.sum(returned.reshape(EXPERTS, PIECES, CAP, D).astype(jnp.float32), axis=1)
        return summed.reshape(EXPERTS * CAP, D)[slot_index]

    grad_flat = cotangent[0].astype(jnp.float32)
    route_inputs = jnp.repeat(normed, TOP, axis=0)
    route_cots = (gates[:, None] * jnp.repeat(grad_flat, TOP, axis=0)).astype(jnp.bfloat16)
    route_rows = jnp.concatenate([route_inputs, route_cots], axis=1)
    width = route_rows.shape[1]
    slots = jnp.zeros((EXPERTS * CAP, width), jnp.bfloat16).at[slot_index].set(route_rows)
    doubled = jnp.broadcast_to(slots.reshape(EXPERTS, 1, CAP, width), (EXPERTS, PIECES, CAP, width))
    both = to_experts(doubled.reshape(senders, local_pieces, CAP, width))
    arrived = both[..., :D]
    arrived_cots = both[..., D:]
    outputs, pre_gate, pre_up, activated, hidden = forward_part(arrived, w_gate, w_up, w_down)
    grad_inputs, grad_gate, grad_up, grad_down = backward_part(
        arrived, arrived_cots, pre_gate, pre_up, activated, hidden, w_gate, w_up, w_down
    )
    returned = to_anchor(jnp.concatenate([outputs, grad_inputs], axis=-1))
    route_out = collect(returned[..., :D])
    route_grad = collect(returned[..., D:])
    moe = jnp.sum((gates[:, None] * route_out).reshape(row_count, TOP, D), axis=1)
    block_out = (stream + moe).astype(jnp.bfloat16)[None]
    grad_unit = jnp.sum(route_grad.reshape(row_count, TOP, D), axis=1)
    grad_stream = (
        grad_flat + (grad_unit - unit * jnp.mean(grad_unit * unit, axis=-1, keepdims=True)) / radius
    )
    return (block_out, grad_stream.astype(jnp.bfloat16)[None], grad_gate, grad_up, grad_down)


def solution(mesh):
    return jax.shard_map(
        body,
        mesh=mesh,
        in_specs=(
            P("table", "blk", None),
            P("table", "blk", None),
            P("table", "blk", None),
            P("table", "blk", None),
            P(),
            P("table", "blk", None),
            P("table", "blk", None),
            P("table", "blk", None),
            P(("table", "blk"), None, None),
            P(("table", "blk"), None, None),
            P(("table", "blk"), None, None),
        ),
        out_specs=(
            P("table", "blk", None),
            P("table", "blk", None),
            P(("table", "blk"), None, None),
            P(("table", "blk"), None, None),
            P(("table", "blk"), None, None),
        ),
        check_vma=False,
    )
```

```python
import math

import jax
import jax.numpy as jnp
from jax import lax
from jax.sharding import PartitionSpec as P

D = 512
HEADS = 8
HEAD = 64
EXPERTS = 64
TOP = 2
PIECES = 2
CAP = 12


def silu_grad(pre):
    sig = jax.nn.sigmoid(pre)
    return sig * (1.0 + pre * (1.0 - sig))


def to_experts(buffer):
    return lax.all_to_all(buffer, ("table", "blk"), split_axis=0, concat_axis=0, tiled=True)


def to_anchor(buffer):
    return lax.all_to_all(buffer, ("table", "blk"), split_axis=0, concat_axis=0, tiled=True)


def forward_part(arrived, w_gate, w_up, w_down):
    pre_gate = jnp.einsum("svcd,vdf->svcf", arrived, w_gate, preferred_element_type=jnp.float32)
    pre_up = jnp.einsum("svcd,vdf->svcf", arrived, w_up, preferred_element_type=jnp.float32)
    activated = jax.nn.silu(pre_gate)
    hidden = (activated * pre_up).astype(jnp.bfloat16)
    outputs = jnp.einsum(
        "svcf,vfd->svcd", hidden, w_down, preferred_element_type=jnp.float32
    ).astype(jnp.bfloat16)
    return (outputs, pre_gate, pre_up, activated, hidden)


def backward_part(arrived, arrived_cots, pre_gate, pre_up, activated, hidden, w_gate, w_up, w_down):
    grad_hidden = jnp.einsum(
        "svcd,vfd->svcf", arrived_cots, w_down, preferred_element_type=jnp.float32
    )
    grad_pre_gate = (grad_hidden * pre_up * silu_grad(pre_gate)).astype(jnp.bfloat16)
    grad_pre_up = (grad_hidden * activated).astype(jnp.bfloat16)
    grad_down = jnp.einsum(
        "svcf,svcd->vfd", hidden, arrived_cots, preferred_element_type=jnp.float32
    ).astype(jnp.bfloat16)
    grad_gate = jnp.einsum(
        "svcd,svcf->vdf", arrived, grad_pre_gate, preferred_element_type=jnp.float32
    ).astype(jnp.bfloat16)
    grad_up = jnp.einsum(
        "svcd,svcf->vdf", arrived, grad_pre_up, preferred_element_type=jnp.float32
    ).astype(jnp.bfloat16)
    grad_inputs = (
        jnp.einsum("svcf,vdf->svcd", grad_pre_gate, w_gate, preferred_element_type=jnp.float32)
        + jnp.einsum("svcf,vdf->svcd", grad_pre_up, w_up, preferred_element_type=jnp.float32)
    ).astype(jnp.bfloat16)
    return (grad_inputs, grad_gate, grad_up, grad_down)


def partner_pairs():
    devices = lax.psum(1, "blk")
    return [(b, b ^ 1) for b in range(devices)]


def dispatch(slots):
    width = slots.shape[1] // PIECES
    parts = jnp.transpose(slots.reshape(EXPERTS, CAP, PIECES, width), (0, 2, 1, 3))
    got = to_experts(parts.reshape(EXPERTS * PIECES, CAP, width))
    other = lax.ppermute(got, "blk", partner_pairs())
    first = lax.axis_index("blk") % 2 == 0
    return jnp.concatenate(
        [jnp.where(first, got, other), jnp.where(first, other, got)], axis=-1
    )


def give_back(outputs, grads):
    first = lax.axis_index("blk") % 2 == 0
    keep = jnp.where(first, outputs, grads)
    other = lax.ppermute(jnp.where(first, grads, outputs), "blk", partner_pairs())
    summed = (keep.astype(jnp.float32) + other.astype(jnp.float32)).astype(jnp.bfloat16)
    back = to_anchor(summed).reshape(EXPERTS, PIECES, CAP, -1)
    return back[:, 0].reshape(EXPERTS * CAP, -1), back[:, 1].reshape(EXPERTS * CAP, -1)


def attend_heads(query_rows, key_rows, value_rows):
    rows = query_rows.shape[0]
    devices = lax.psum(1, "blk")
    groups = devices // HEADS
    part = rows // groups
    scale = 1.0 / math.sqrt(HEAD)

    def by_head(block):
        heads = jnp.transpose(block.reshape(rows, HEADS, HEAD), (1, 0, 2))
        return jnp.broadcast_to(heads[:, None], (HEADS, groups, rows, HEAD)).reshape(devices, rows, HEAD)

    pairs = jnp.concatenate([by_head(key_rows), by_head(value_rows)], axis=-1)
    asked = jnp.transpose(query_rows.reshape(groups, part, HEADS, HEAD), (2, 0, 1, 3))
    asked = asked.reshape(devices, part, HEAD)
    asked = jnp.concatenate([asked, jnp.zeros_like(asked)], axis=-1)
    parcel = jnp.concatenate([pairs, asked], axis=1)
    got = lax.all_to_all(parcel, "blk", 0, 0, tiled=True)
    keys = got[:, :rows, :HEAD].reshape(devices * rows, HEAD)
    values = got[:, :rows, HEAD:].reshape(devices * rows, HEAD)
    mine = got[:, rows:, :HEAD].reshape(devices * part, HEAD)
    scores = jnp.dot(mine, keys.T, preferred_element_type=jnp.float32) * scale
    highest = jnp.max(scores, axis=-1, keepdims=True)
    expo = jnp.exp(scores - highest)
    denom = jnp.sum(expo, axis=-1, keepdims=True)
    totals = jnp.dot(expo.astype(jnp.bfloat16), values, preferred_element_type=jnp.float32)
    mixed = (totals / denom).astype(jnp.bfloat16).reshape(devices, part, HEAD)
    back = lax.all_to_all(mixed, "blk", 0, 0, tiled=True)
    back = jnp.transpose(back.reshape(HEADS, groups, part, HEAD), (1, 2, 0, 3))
    return back.reshape(rows, HEADS * HEAD)


def body(
    residual,
    queries,
    key_rows,
    value_rows,
    w_out,
    expert_ids,
    route_gates,
    cotangent,
    w_gate,
    w_up,
    w_down,
):
    row_count = queries.shape[1]
    route_experts = expert_ids[0].reshape(-1)
    gates = route_gates[0].reshape(-1)
    onehot = (route_experts[:, None] == jnp.arange(EXPERTS, dtype=jnp.int32)[None, :]).astype(
        jnp.int32
    )
    before = jnp.cumsum(onehot, axis=0) - onehot
    position = jnp.sum(before * onehot, axis=1)
    slot_index = route_experts * CAP + position
    grad_flat = cotangent[0].astype(jnp.float32)
    route_cots = (gates[:, None] * jnp.repeat(grad_flat, TOP, axis=0)).astype(jnp.bfloat16)
    cot_slots = jnp.zeros((EXPERTS * CAP, D), jnp.bfloat16).at[slot_index].set(route_cots)
    arrived_cots = dispatch(cot_slots).reshape(-1, w_gate.shape[0], CAP, D)
    attended = attend_heads(queries[0], key_rows[0], value_rows[0])
    stream = residual[0].astype(jnp.float32) + jnp.dot(
        attended, w_out, preferred_element_type=jnp.float32
    )
    radius = jnp.sqrt(jnp.mean(stream * stream, axis=-1, keepdims=True) + 1e-06)
    unit = stream / radius
    normed = unit.astype(jnp.bfloat16)
    local_pieces = w_gate.shape[0]
    in_slots = jnp.zeros((EXPERTS * CAP, D), jnp.bfloat16).at[slot_index].set(
        jnp.repeat(normed, TOP, axis=0)
    )
    arrived = dispatch(in_slots).reshape(-1, local_pieces, CAP, D)
    outputs, pre_gate, pre_up, activated, hidden = forward_part(arrived, w_gate, w_up, w_down)
    grad_inputs, grad_gate, grad_up, grad_down = backward_part(
        arrived, arrived_cots, pre_gate, pre_up, activated, hidden, w_gate, w_up, w_down
    )
    out_slots, grad_slots = give_back(outputs[:, 0], grad_inputs[:, 0])
    route_out = out_slots.astype(jnp.float32)[slot_index]
    route_grad = grad_slots.astype(jnp.float32)[slot_index]
    moe = jnp.sum((gates[:, None] * route_out).reshape(row_count, TOP, D), axis=1)
    block_out = (stream + moe).astype(jnp.bfloat16)[None]
    grad_unit = jnp.sum(route_grad.reshape(row_count, TOP, D), axis=1)
    grad_stream = (
        grad_flat + (grad_unit - unit * jnp.mean(grad_unit * unit, axis=-1, keepdims=True)) / radius
    )
    return (block_out, grad_stream.astype(jnp.bfloat16)[None], grad_gate, grad_up, grad_down)


def solution(mesh):
    return jax.shard_map(
        body,
        mesh=mesh,
        in_specs=(
            P("table", "blk", None),
            P("table", "blk", None),
            P("table", "blk", None),
            P("table", "blk", None),
            P(),
            P("table", "blk", None),
            P("table", "blk", None),
            P("table", "blk", None),
            P(("table", "blk"), None, None),
            P(("table", "blk"), None, None),
            P(("table", "blk"), None, None),
        ),
        out_specs=(
            P("table", "blk", None),
            P("table", "blk", None),
            P(("table", "blk"), None, None),
            P(("table", "blk"), None, None),
            P(("table", "blk"), None, None),
        ),
        check_vma=False,
    )
```

```python
import math

import jax
import jax.numpy as jnp
from jax import lax
from jax.experimental import pallas as pl
from jax.experimental.pallas import tpu as pltpu
from jax.sharding import PartitionSpec as P


D = 512
HEADS = 8
HEAD = 64
EXPERTS = 64
TOP = 2
PIECES = 2
CAP = 12


def silu_grad(pre):
    sig = jax.nn.sigmoid(pre)
    return sig * (1.0 + pre * (1.0 - sig))


def to_experts(buffer):
    return lax.all_to_all(buffer, ("table", "blk"), split_axis=0, concat_axis=0, tiled=True)


def to_anchor(buffer):
    return lax.all_to_all(buffer, ("table", "blk"), split_axis=0, concat_axis=0, tiled=True)


def forward_part(arrived, w_gate, w_up, w_down):
    pre_gate = jnp.einsum("svcd,vdf->svcf", arrived, w_gate, preferred_element_type=jnp.float32)
    pre_up = jnp.einsum("svcd,vdf->svcf", arrived, w_up, preferred_element_type=jnp.float32)
    activated = jax.nn.silu(pre_gate)
    hidden = (activated * pre_up).astype(jnp.bfloat16)
    outputs = jnp.einsum(
        "svcf,vfd->svcd", hidden, w_down, preferred_element_type=jnp.float32
    ).astype(jnp.bfloat16)
    return (outputs, pre_gate, pre_up, activated, hidden)


def backward_part(arrived, arrived_cots, pre_gate, pre_up, activated, hidden, w_gate, w_up, w_down):
    grad_hidden = jnp.einsum(
        "svcd,vfd->svcf", arrived_cots, w_down, preferred_element_type=jnp.float32
    )
    grad_pre_gate = (grad_hidden * pre_up * silu_grad(pre_gate)).astype(jnp.bfloat16)
    grad_pre_up = (grad_hidden * activated).astype(jnp.bfloat16)
    grad_down = jnp.einsum(
        "svcf,svcd->vfd", hidden, arrived_cots, preferred_element_type=jnp.float32
    ).astype(jnp.bfloat16)
    grad_gate = jnp.einsum(
        "svcd,svcf->vdf", arrived, grad_pre_gate, preferred_element_type=jnp.float32
    ).astype(jnp.bfloat16)
    grad_up = jnp.einsum(
        "svcd,svcf->vdf", arrived, grad_pre_up, preferred_element_type=jnp.float32
    ).astype(jnp.bfloat16)
    grad_inputs = (
        jnp.einsum("svcf,vdf->svcd", grad_pre_gate, w_gate, preferred_element_type=jnp.float32)
        + jnp.einsum("svcf,vdf->svcd", grad_pre_up, w_up, preferred_element_type=jnp.float32)
    ).astype(jnp.bfloat16)
    return (grad_inputs, grad_gate, grad_up, grad_down)


def partner_pairs():
    devices = lax.psum(1, "blk")
    return [(b, b ^ 1) for b in range(devices)]


def dispatch(slots):
    width = slots.shape[1] // PIECES
    parts = jnp.transpose(slots.reshape(EXPERTS, CAP, PIECES, width), (0, 2, 1, 3))
    got = to_experts(parts.reshape(EXPERTS * PIECES, CAP, width))
    other = lax.ppermute(got, "blk", partner_pairs())
    first = lax.axis_index("blk") % 2 == 0
    return jnp.concatenate(
        [jnp.where(first, got, other), jnp.where(first, other, got)], axis=-1
    )


def give_back(outputs, grads):
    first = lax.axis_index("blk") % 2 == 0
    keep = jnp.where(first, outputs, grads)
    other = lax.ppermute(jnp.where(first, grads, outputs), "blk", partner_pairs())
    summed = (keep.astype(jnp.float32) + other.astype(jnp.float32)).astype(jnp.bfloat16)
    back = to_anchor(summed).reshape(EXPERTS, PIECES, CAP, -1)
    return back[:, 0].reshape(EXPERTS * CAP, -1), back[:, 1].reshape(EXPERTS * CAP, -1)


def attend_heads(query_rows, key_rows, value_rows):
    rows = query_rows.shape[0]
    devices = lax.psum(1, "blk")
    groups = devices // HEADS
    part = rows // groups
    scale = 1.0 / math.sqrt(HEAD)

    def by_head(block):
        heads = jnp.transpose(block.reshape(rows, HEADS, HEAD), (1, 0, 2))
        return jnp.broadcast_to(heads[:, None], (HEADS, groups, rows, HEAD)).reshape(devices, rows, HEAD)

    pairs = jnp.concatenate([by_head(key_rows), by_head(value_rows)], axis=-1)
    asked = jnp.transpose(query_rows.reshape(groups, part, HEADS, HEAD), (2, 0, 1, 3))
    asked = asked.reshape(devices, part, HEAD)
    asked = jnp.concatenate([asked, jnp.zeros_like(asked)], axis=-1)
    parcel = jnp.concatenate([pairs, asked], axis=1)
    got = lax.all_to_all(parcel, "blk", 0, 0, tiled=True)
    steps = 4
    chunk = devices // steps

    def kernel(got_ref, out_ref):
        step = pl.program_id(0)
        pairs_all = got_ref[:, :rows, :].reshape(devices * rows, 2 * HEAD)
        asked_now = got_ref[pl.ds(step * chunk, chunk), rows:, :].reshape(chunk * part, 2 * HEAD)
        scores = lax.dot_general(
            asked_now, pairs_all, (((1,), (1,)), ((), ())), preferred_element_type=jnp.float32
        ) * scale
        highest = jnp.max(scores, axis=-1, keepdims=True)
        expo = jnp.exp(scores - highest)
        denom = jnp.sum(expo, axis=-1, keepdims=True)
        totals = jnp.dot(expo.astype(jnp.bfloat16), pairs_all, preferred_element_type=jnp.float32)
        out_ref[...] = (totals[:, HEAD:] / denom).astype(jnp.bfloat16).reshape(chunk, part, HEAD)

    queries_total = devices * part
    keys_total = devices * rows
    mixed = pl.pallas_call(
        kernel,
        grid=(steps,),
        in_specs=[pl.BlockSpec(got.shape, lambda i: (0, 0, 0))],
        out_specs=pl.BlockSpec((chunk, part, HEAD), lambda i: (i, 0, 0)),
        out_shape=jax.ShapeDtypeStruct((devices, part, HEAD), jnp.bfloat16),
        compiler_params=pltpu.CompilerParams(vmem_limit_bytes=48 * 1024 * 1024),
        cost_estimate=pl.CostEstimate(
            flops=4 * queries_total * keys_total * 2 * HEAD,
            transcendentals=queries_total * keys_total,
            bytes_accessed=got.size * 2 + queries_total * HEAD * 2,
        ),
    )(got)
    back = lax.all_to_all(mixed, "blk", 0, 0, tiled=True)
    back = jnp.transpose(back.reshape(HEADS, groups, part, HEAD), (1, 2, 0, 3))
    return back.reshape(rows, HEADS * HEAD)


def block(
    residual,
    queries,
    key_rows,
    value_rows,
    w_out,
    expert_ids,
    route_gates,
    cotangent,
    w_gate,
    w_up,
    w_down,
):
    row_count = queries.shape[1]
    route_experts = expert_ids[0].reshape(-1)
    gates = route_gates[0].reshape(-1)
    onehot = (route_experts[:, None] == jnp.arange(EXPERTS, dtype=jnp.int32)[None, :]).astype(
        jnp.int32
    )
    before = jnp.cumsum(onehot, axis=0) - onehot
    position = jnp.sum(before * onehot, axis=1)
    slot_index = route_experts * CAP + position
    grad_flat = cotangent[0].astype(jnp.float32)
    route_cots = (gates[:, None] * jnp.repeat(grad_flat, TOP, axis=0)).astype(jnp.bfloat16)
    cot_slots = jnp.zeros((EXPERTS * CAP, D), jnp.bfloat16).at[slot_index].set(route_cots)
    arrived_cots = dispatch(cot_slots).reshape(-1, w_gate.shape[0], CAP, D)
    attended = attend_heads(queries[0], key_rows[0], value_rows[0])
    stream = residual[0].astype(jnp.float32) + jnp.dot(
        attended, w_out, preferred_element_type=jnp.float32
    )
    radius = jnp.sqrt(jnp.mean(stream * stream, axis=-1, keepdims=True) + 1e-06)
    unit = stream / radius
    normed = unit.astype(jnp.bfloat16)
    local_pieces = w_gate.shape[0]
    in_slots = jnp.zeros((EXPERTS * CAP, D), jnp.bfloat16).at[slot_index].set(
        jnp.repeat(normed, TOP, axis=0)
    )
    arrived = dispatch(in_slots).reshape(-1, local_pieces, CAP, D)
    outputs, pre_gate, pre_up, activated, hidden = forward_part(arrived, w_gate, w_up, w_down)
    grad_inputs, grad_gate, grad_up, grad_down = backward_part(
        arrived, arrived_cots, pre_gate, pre_up, activated, hidden, w_gate, w_up, w_down
    )
    out_slots, grad_slots = give_back(outputs[:, 0], grad_inputs[:, 0])
    route_out = out_slots.astype(jnp.float32)[slot_index]
    route_grad = grad_slots.astype(jnp.float32)[slot_index]
    moe = jnp.sum((gates[:, None] * route_out).reshape(row_count, TOP, D), axis=1)
    block_out = (stream + moe).astype(jnp.bfloat16)[None]
    grad_unit = jnp.sum(route_grad.reshape(row_count, TOP, D), axis=1)
    grad_stream = (
        grad_flat + (grad_unit - unit * jnp.mean(grad_unit * unit, axis=-1, keepdims=True)) / radius
    )
    return (block_out, grad_stream.astype(jnp.bfloat16)[None], grad_gate, grad_up, grad_down)


def solution(mesh):
    return jax.shard_map(
        block,
        mesh=mesh,
        in_specs=(
            P("table", "blk", None),
            P("table", "blk", None),
            P("table", "blk", None),
            P("table", "blk", None),
            P(),
            P("table", "blk", None),
            P("table", "blk", None),
            P("table", "blk", None),
            P(("table", "blk"), None, None),
            P(("table", "blk"), None, None),
            P(("table", "blk"), None, None),
        ),
        out_specs=(
            P("table", "blk", None),
            P("table", "blk", None),
            P(("table", "blk"), None, None),
            P(("table", "blk"), None, None),
            P(("table", "blk"), None, None),
        ),
        check_vma=False,
    )
```

```python
import math

import jax
import jax.numpy as jnp
from jax import lax
from jax.experimental import pallas as pl
from jax.experimental.pallas import tpu as pltpu
from jax.sharding import PartitionSpec as P


D = 512
HEADS = 8
HEAD = 64
EXPERTS = 64
TOP = 2
PIECES = 2
CAP = 12


def silu_grad(pre):
    sig = jax.nn.sigmoid(pre)
    return sig * (1.0 + pre * (1.0 - sig))


def to_experts(buffer):
    return lax.all_to_all(buffer, ("table", "blk"), split_axis=0, concat_axis=0, tiled=True)


def to_anchor(buffer):
    return lax.all_to_all(buffer, ("table", "blk"), split_axis=0, concat_axis=0, tiled=True)


def partner_pairs():
    devices = lax.psum(1, "blk")
    return [(b, b ^ 1) for b in range(devices)]


def spread(slots):
    half = CAP // PIECES
    got = to_experts(slots.reshape(EXPERTS * PIECES, half, slots.shape[1]))
    other = lax.ppermute(got, "blk", partner_pairs())
    return got.reshape(-1, slots.shape[1]), other.reshape(-1, slots.shape[1])


def piece_pass(inputs, cots, gate_mat, up_mat, down_mat):
    pre_gate = jnp.dot(inputs, gate_mat, preferred_element_type=jnp.float32)
    pre_up = jnp.dot(inputs, up_mat, preferred_element_type=jnp.float32)
    activated = jax.nn.silu(pre_gate)
    hidden = (activated * pre_up).astype(jnp.bfloat16)
    output = jnp.dot(hidden, down_mat, preferred_element_type=jnp.float32).astype(jnp.bfloat16)
    grad_hidden = jnp.dot(cots, down_mat.T, preferred_element_type=jnp.float32)
    grad_pre_gate = (grad_hidden * pre_up * silu_grad(pre_gate)).astype(jnp.bfloat16)
    grad_pre_up = (grad_hidden * activated).astype(jnp.bfloat16)
    grad_inputs = (
        jnp.dot(grad_pre_gate, gate_mat.T, preferred_element_type=jnp.float32)
        + jnp.dot(grad_pre_up, up_mat.T, preferred_element_type=jnp.float32)
    ).astype(jnp.bfloat16)
    grad_down = jnp.dot(hidden.T, cots, preferred_element_type=jnp.float32)
    grad_gate = jnp.dot(inputs.T, grad_pre_gate, preferred_element_type=jnp.float32)
    grad_up = jnp.dot(inputs.T, grad_pre_up, preferred_element_type=jnp.float32)
    return (jnp.concatenate([output, grad_inputs], axis=-1), grad_gate, grad_up, grad_down)


def attend_heads(query_rows, key_rows, value_rows):
    rows = query_rows.shape[0]
    devices = lax.psum(1, "blk")
    groups = devices // HEADS
    part = rows // groups
    scale = 1.0 / math.sqrt(HEAD)

    def by_head(block):
        heads = jnp.transpose(block.reshape(rows, HEADS, HEAD), (1, 0, 2))
        return jnp.broadcast_to(heads[:, None], (HEADS, groups, rows, HEAD)).reshape(devices, rows, HEAD)

    pairs = jnp.concatenate([by_head(key_rows), by_head(value_rows)], axis=-1)
    asked = jnp.transpose(query_rows.reshape(groups, part, HEADS, HEAD), (2, 0, 1, 3))
    asked = asked.reshape(devices, part, HEAD)
    asked = jnp.concatenate([asked, jnp.zeros_like(asked)], axis=-1)
    parcel = jnp.concatenate([pairs, asked], axis=1)
    got = lax.all_to_all(parcel, "blk", 0, 0, tiled=True)
    steps = 4
    chunk = devices // steps

    def kernel(got_ref, out_ref):
        step = pl.program_id(0)
        pairs_all = got_ref[:, :rows, :].reshape(devices * rows, 2 * HEAD)
        asked_now = got_ref[pl.ds(step * chunk, chunk), rows:, :].reshape(chunk * part, 2 * HEAD)
        scores = lax.dot_general(
            asked_now, pairs_all, (((1,), (1,)), ((), ())), preferred_element_type=jnp.float32
        ) * scale
        highest = jnp.max(scores, axis=-1, keepdims=True)
        expo = jnp.exp(scores - highest)
        denom = jnp.sum(expo, axis=-1, keepdims=True)
        totals = jnp.dot(expo.astype(jnp.bfloat16), pairs_all, preferred_element_type=jnp.float32)
        out_ref[...] = (totals[:, HEAD:] / denom).astype(jnp.bfloat16).reshape(chunk, part, HEAD)

    queries_total = devices * part
    keys_total = devices * rows
    mixed = pl.pallas_call(
        kernel,
        grid=(steps,),
        in_specs=[pl.BlockSpec(got.shape, lambda i: (0, 0, 0))],
        out_specs=pl.BlockSpec((chunk, part, HEAD), lambda i: (i, 0, 0)),
        out_shape=jax.ShapeDtypeStruct((devices, part, HEAD), jnp.bfloat16),
        compiler_params=pltpu.CompilerParams(vmem_limit_bytes=48 * 1024 * 1024),
        cost_estimate=pl.CostEstimate(
            flops=4 * queries_total * keys_total * 2 * HEAD,
            transcendentals=queries_total * keys_total,
            bytes_accessed=got.size * 2 + queries_total * HEAD * 2,
        ),
    )(got)
    back = lax.all_to_all(mixed, "blk", 0, 0, tiled=True)
    back = jnp.transpose(back.reshape(HEADS, groups, part, HEAD), (1, 2, 0, 3))
    return back.reshape(rows, HEADS * HEAD)


def block(
    residual,
    queries,
    key_rows,
    value_rows,
    w_out,
    expert_ids,
    route_gates,
    cotangent,
    w_gate,
    w_up,
    w_down,
):
    row_count = queries.shape[1]
    route_experts = expert_ids[0].reshape(-1)
    gates = route_gates[0].reshape(-1)
    onehot = (route_experts[:, None] == jnp.arange(EXPERTS, dtype=jnp.int32)[None, :]).astype(
        jnp.int32
    )
    before = jnp.cumsum(onehot, axis=0) - onehot
    position = jnp.sum(before * onehot, axis=1)
    slot_index = route_experts * CAP + position
    grad_flat = cotangent[0].astype(jnp.float32)
    route_cots = (gates[:, None] * jnp.repeat(grad_flat, TOP, axis=0)).astype(jnp.bfloat16)
    slot_ids = jnp.arange(EXPERTS * CAP, dtype=jnp.int32)
    placing = (slot_ids[:, None] == slot_index[None, :]).astype(jnp.bfloat16)
    cot_slots = jnp.dot(placing, route_cots, preferred_element_type=jnp.float32).astype(jnp.bfloat16)
    cot_own, cot_other = spread(cot_slots)
    attended = attend_heads(queries[0], key_rows[0], value_rows[0])
    stream = residual[0].astype(jnp.float32) + jnp.dot(
        attended, w_out, preferred_element_type=jnp.float32
    )
    radius = jnp.sqrt(jnp.mean(stream * stream, axis=-1, keepdims=True) + 1e-06)
    unit = stream / radius
    normed = unit.astype(jnp.bfloat16)
    in_slots = jnp.dot(
        placing, jnp.repeat(normed, TOP, axis=0), preferred_element_type=jnp.float32
    ).astype(jnp.bfloat16)
    in_own, in_other = spread(in_slots)
    mats = (w_gate[0], w_up[0], w_down[0])
    own, gate_a, up_a, down_a = piece_pass(in_own, cot_own, *mats)
    other, gate_b, up_b, down_b = piece_pass(in_other, cot_other, *mats)
    theirs = lax.ppermute(other, "blk", partner_pairs())
    summed = (own.astype(jnp.float32) + theirs.astype(jnp.float32)).astype(jnp.bfloat16)
    back = to_anchor(summed.reshape(EXPERTS * PIECES, CAP // PIECES, 2 * D))
    picking = (slot_index[:, None] == slot_ids[None, :]).astype(jnp.bfloat16)
    picked = jnp.dot(picking, back.reshape(EXPERTS * CAP, 2 * D), preferred_element_type=jnp.float32)
    route_out = picked[:, :D]
    route_grad = picked[:, D:]
    grad_gate = (gate_a + gate_b).astype(jnp.bfloat16)[None]
    grad_up = (up_a + up_b).astype(jnp.bfloat16)[None]
    grad_down = (down_a + down_b).astype(jnp.bfloat16)[None]
    moe = jnp.sum((gates[:, None] * route_out).reshape(row_count, TOP, D), axis=1)
    block_out = (stream + moe).astype(jnp.bfloat16)[None]
    grad_unit = jnp.sum(route_grad.reshape(row_count, TOP, D), axis=1)
    grad_stream = (
        grad_flat + (grad_unit - unit * jnp.mean(grad_unit * unit, axis=-1, keepdims=True)) / radius
    )
    return (block_out, grad_stream.astype(jnp.bfloat16)[None], grad_gate, grad_up, grad_down)


def solution(mesh):
    return jax.shard_map(
        block,
        mesh=mesh,
        in_specs=(
            P("table", "blk", None),
            P("table", "blk", None),
            P("table", "blk", None),
            P("table", "blk", None),
            P(),
            P("table", "blk", None),
            P("table", "blk", None),
            P("table", "blk", None),
            P(("table", "blk"), None, None),
            P(("table", "blk"), None, None),
            P(("table", "blk"), None, None),
        ),
        out_specs=(
            P("table", "blk", None),
            P("table", "blk", None),
            P(("table", "blk"), None, None),
            P(("table", "blk"), None, None),
            P(("table", "blk"), None, None),
        ),
        check_vma=False,
    )
```

```python
import math

import jax
import jax.numpy as jnp
from jax import lax
from jax.experimental import pallas as pl
from jax.experimental.pallas import tpu as pltpu
from jax.sharding import PartitionSpec as P


D = 512
HEADS = 8
HEAD = 64
EXPERTS = 64
TOP = 2
PIECES = 2
CAP = 12


def silu_grad(pre):
    sig = jax.nn.sigmoid(pre)
    return sig * (1.0 + pre * (1.0 - sig))


def to_experts(buffer):
    return lax.all_to_all(buffer, ("table", "blk"), split_axis=0, concat_axis=0, tiled=True)


def to_anchor(buffer):
    return lax.all_to_all(buffer, ("table", "blk"), split_axis=0, concat_axis=0, tiled=True)


def partner_pairs():
    devices = lax.psum(1, "blk")
    return [(b, b ^ 1) for b in range(devices)]


def spread(slots):
    got = to_experts(slots)
    other = lax.ppermute(got, "blk", partner_pairs())
    return got, other


def piece_pass(inputs, cots, gate_mat, up_mat, down_mat):
    pre_gate = jnp.einsum("scd,df->scf", inputs, gate_mat, preferred_element_type=jnp.float32)
    pre_up = jnp.einsum("scd,df->scf", inputs, up_mat, preferred_element_type=jnp.float32)
    activated = jax.nn.silu(pre_gate)
    hidden = (activated * pre_up).astype(jnp.bfloat16)
    output = jnp.einsum(
        "scf,fd->scd", hidden, down_mat, preferred_element_type=jnp.float32
    ).astype(jnp.bfloat16)
    grad_hidden = jnp.einsum("scd,fd->scf", cots, down_mat, preferred_element_type=jnp.float32)
    grad_pre_gate = (grad_hidden * pre_up * silu_grad(pre_gate)).astype(jnp.bfloat16)
    grad_pre_up = (grad_hidden * activated).astype(jnp.bfloat16)
    grad_inputs = (
        jnp.einsum("scf,df->scd", grad_pre_gate, gate_mat, preferred_element_type=jnp.float32)
        + jnp.einsum("scf,df->scd", grad_pre_up, up_mat, preferred_element_type=jnp.float32)
    ).astype(jnp.bfloat16)
    grad_down = jnp.einsum("scf,scd->fd", hidden, cots, preferred_element_type=jnp.float32)
    grad_gate = jnp.einsum("scd,scf->df", inputs, grad_pre_gate, preferred_element_type=jnp.float32)
    grad_up = jnp.einsum("scd,scf->df", inputs, grad_pre_up, preferred_element_type=jnp.float32)
    return (jnp.concatenate([output, grad_inputs], axis=-1), grad_gate, grad_up, grad_down)


def attend_heads(query_rows, key_rows, value_rows):
    rows = query_rows.shape[0]
    devices = lax.psum(1, "blk")
    groups = devices // HEADS
    part = rows // groups
    scale = 1.0 / math.sqrt(HEAD)

    def by_head(block):
        heads = jnp.transpose(block.reshape(rows, HEADS, HEAD), (1, 0, 2))
        return jnp.broadcast_to(heads[:, None], (HEADS, groups, rows, HEAD)).reshape(devices, rows, HEAD)

    pairs = jnp.concatenate([by_head(key_rows), by_head(value_rows)], axis=-1)
    asked = jnp.transpose(query_rows.reshape(groups, part, HEADS, HEAD), (2, 0, 1, 3))
    asked = asked.reshape(devices, part, HEAD)
    asked = jnp.concatenate([asked, jnp.zeros_like(asked)], axis=-1)
    parcel = jnp.concatenate([pairs, asked], axis=1)
    got = lax.all_to_all(parcel, "blk", 0, 0, tiled=True)
    steps = 4
    chunk = devices // steps

    def kernel(got_ref, out_ref):
        step = pl.program_id(0)
        pairs_all = got_ref[:, :rows, :].reshape(devices * rows, 2 * HEAD)
        asked_now = got_ref[pl.ds(step * chunk, chunk), rows:, :].reshape(chunk * part, 2 * HEAD)
        scores = lax.dot_general(
            asked_now, pairs_all, (((1,), (1,)), ((), ())), preferred_element_type=jnp.float32
        ) * scale
        highest = jnp.max(scores, axis=-1, keepdims=True)
        expo = jnp.exp(scores - highest)
        denom = jnp.sum(expo, axis=-1, keepdims=True)
        totals = jnp.dot(expo.astype(jnp.bfloat16), pairs_all, preferred_element_type=jnp.float32)
        out_ref[...] = (totals[:, HEAD:] / denom).astype(jnp.bfloat16).reshape(chunk, part, HEAD)

    queries_total = devices * part
    keys_total = devices * rows
    mixed = pl.pallas_call(
        kernel,
        grid=(steps,),
        in_specs=[pl.BlockSpec(got.shape, lambda i: (0, 0, 0))],
        out_specs=pl.BlockSpec((chunk, part, HEAD), lambda i: (i, 0, 0)),
        out_shape=jax.ShapeDtypeStruct((devices, part, HEAD), jnp.bfloat16),
        compiler_params=pltpu.CompilerParams(vmem_limit_bytes=48 * 1024 * 1024),
        cost_estimate=pl.CostEstimate(
            flops=4 * queries_total * keys_total * 2 * HEAD,
            transcendentals=queries_total * keys_total,
            bytes_accessed=got.size * 2 + queries_total * HEAD * 2,
        ),
    )(got)
    back = lax.all_to_all(mixed, "blk", 0, 0, tiled=True)
    back = jnp.transpose(back.reshape(HEADS, groups, part, HEAD), (1, 2, 0, 3))
    return back.reshape(rows, HEADS * HEAD)


def block(
    residual,
    queries,
    key_rows,
    value_rows,
    w_out,
    expert_ids,
    route_gates,
    cotangent,
    w_gate,
    w_up,
    w_down,
):
    row_count = queries.shape[1]
    route_experts = expert_ids[0].reshape(-1)
    gates = route_gates[0].reshape(-1)
    onehot = (route_experts[:, None] == jnp.arange(EXPERTS, dtype=jnp.int32)[None, :]).astype(
        jnp.int32
    )
    before = jnp.cumsum(onehot, axis=0) - onehot
    position = jnp.sum(before * onehot, axis=1)
    slot_index = route_experts * CAP + position
    grad_flat = cotangent[0].astype(jnp.float32)
    route_cots = (gates[:, None] * jnp.repeat(grad_flat, TOP, axis=0)).astype(jnp.bfloat16)
    half = CAP // PIECES
    slot_ids = jnp.arange(EXPERTS * CAP, dtype=jnp.int32).reshape(EXPERTS * PIECES, half)
    placing = (slot_ids[:, :, None] == slot_index[None, None, :]).astype(jnp.bfloat16)
    cot_slots = jnp.einsum(
        "jcr,rw->jcw", placing, route_cots, preferred_element_type=jnp.float32
    ).astype(jnp.bfloat16)
    cot_own, cot_other = spread(cot_slots)
    attended = attend_heads(queries[0], key_rows[0], value_rows[0])
    stream = residual[0].astype(jnp.float32) + jnp.dot(
        attended, w_out, preferred_element_type=jnp.float32
    )
    radius = jnp.sqrt(jnp.mean(stream * stream, axis=-1, keepdims=True) + 1e-06)
    unit = stream / radius
    normed = unit.astype(jnp.bfloat16)
    in_slots = jnp.einsum(
        "jcr,rw->jcw", placing, jnp.repeat(normed, TOP, axis=0), preferred_element_type=jnp.float32
    ).astype(jnp.bfloat16)
    in_own, in_other = spread(in_slots)
    mats = (w_gate[0], w_up[0], w_down[0])
    own, gate_a, up_a, down_a = piece_pass(in_own, cot_own, *mats)
    other, gate_b, up_b, down_b = piece_pass(in_other, cot_other, *mats)
    theirs = lax.ppermute(other, "blk", partner_pairs())
    summed = (own.astype(jnp.float32) + theirs.astype(jnp.float32)).astype(jnp.bfloat16)
    back = to_anchor(summed)
    picking = (slot_index[:, None, None] == slot_ids[None, :, :]).astype(jnp.bfloat16)
    picked = jnp.einsum("rjc,jcw->rw", picking, back, preferred_element_type=jnp.float32)
    route_out = picked[:, :D]
    route_grad = picked[:, D:]
    grad_gate = (gate_a + gate_b).astype(jnp.bfloat16)[None]
    grad_up = (up_a + up_b).astype(jnp.bfloat16)[None]
    grad_down = (down_a + down_b).astype(jnp.bfloat16)[None]
    moe = jnp.sum((gates[:, None] * route_out).reshape(row_count, TOP, D), axis=1)
    block_out = (stream + moe).astype(jnp.bfloat16)[None]
    grad_unit = jnp.sum(route_grad.reshape(row_count, TOP, D), axis=1)
    grad_stream = (
        grad_flat + (grad_unit - unit * jnp.mean(grad_unit * unit, axis=-1, keepdims=True)) / radius
    )
    return (block_out, grad_stream.astype(jnp.bfloat16)[None], grad_gate, grad_up, grad_down)


def solution(mesh):
    return jax.shard_map(
        block,
        mesh=mesh,
        in_specs=(
            P("table", "blk", None),
            P("table", "blk", None),
            P("table", "blk", None),
            P("table", "blk", None),
            P(),
            P("table", "blk", None),
            P("table", "blk", None),
            P("table", "blk", None),
            P(("table", "blk"), None, None),
            P(("table", "blk"), None, None),
            P(("table", "blk"), None, None),
        ),
        out_specs=(
            P("table", "blk", None),
            P("table", "blk", None),
            P(("table", "blk"), None, None),
            P(("table", "blk"), None, None),
            P(("table", "blk"), None, None),
        ),
        check_vma=False,
    )
```

```python
import math

import jax
import jax.numpy as jnp
from jax import lax
from jax.experimental import pallas as pl
from jax.experimental.pallas import tpu as pltpu
from jax.sharding import PartitionSpec as P


D = 512
HEADS = 8
HEAD = 64
EXPERTS = 64
TOP = 2
PIECES = 2
CAP = 12


def silu_grad(pre):
    sig = jax.nn.sigmoid(pre)
    return sig * (1.0 + pre * (1.0 - sig))


def to_experts(buffer):
    return lax.all_to_all(buffer, ("table", "blk"), split_axis=0, concat_axis=0, tiled=True)


def to_anchor(buffer):
    return lax.all_to_all(buffer, ("table", "blk"), split_axis=0, concat_axis=0, tiled=True)


def partner_pairs():
    devices = lax.psum(1, "blk")
    return [(b, b ^ 1) for b in range(devices)]


def spread(slots):
    got = to_experts(slots)
    other = lax.ppermute(got, "blk", partner_pairs())
    return got, other


def piece_pass(inputs, cots, gate_mat, up_mat, down_mat):
    pre_gate = jnp.einsum("scd,df->scf", inputs, gate_mat, preferred_element_type=jnp.float32)
    pre_up = jnp.einsum("scd,df->scf", inputs, up_mat, preferred_element_type=jnp.float32)
    activated = jax.nn.silu(pre_gate)
    hidden = (activated * pre_up).astype(jnp.bfloat16)
    output = jnp.einsum(
        "scf,fd->scd", hidden, down_mat, preferred_element_type=jnp.float32
    ).astype(jnp.bfloat16)
    grad_hidden = jnp.einsum("scd,fd->scf", cots, down_mat, preferred_element_type=jnp.float32)
    grad_pre_gate = (grad_hidden * pre_up * silu_grad(pre_gate)).astype(jnp.bfloat16)
    grad_pre_up = (grad_hidden * activated).astype(jnp.bfloat16)
    grad_inputs = (
        jnp.einsum("scf,df->scd", grad_pre_gate, gate_mat, preferred_element_type=jnp.float32)
        + jnp.einsum("scf,df->scd", grad_pre_up, up_mat, preferred_element_type=jnp.float32)
    ).astype(jnp.bfloat16)
    grad_down = jnp.einsum("scf,scd->fd", hidden, cots, preferred_element_type=jnp.float32)
    grad_gate = jnp.einsum("scd,scf->df", inputs, grad_pre_gate, preferred_element_type=jnp.float32)
    grad_up = jnp.einsum("scd,scf->df", inputs, grad_pre_up, preferred_element_type=jnp.float32)
    return (jnp.concatenate([output, grad_inputs], axis=-1), grad_gate, grad_up, grad_down)


def attend_heads(query_rows, key_rows, value_rows):
    rows = query_rows.shape[0]
    devices = lax.psum(1, "blk")
    groups = devices // HEADS
    part = rows // groups
    scale = 1.0 / math.sqrt(HEAD)

    def by_head(block):
        heads = jnp.transpose(block.reshape(rows, HEADS, HEAD), (1, 0, 2))
        return jnp.broadcast_to(heads[:, None], (HEADS, groups, rows, HEAD)).reshape(devices, rows, HEAD)

    pairs = jnp.concatenate([by_head(key_rows), by_head(value_rows)], axis=-1)
    asked = jnp.transpose(query_rows.reshape(groups, part, HEADS, HEAD), (2, 0, 1, 3))
    asked = asked.reshape(devices, part, HEAD)
    asked = jnp.concatenate([asked, jnp.zeros_like(asked)], axis=-1)
    parcel = jnp.concatenate([pairs, asked], axis=1)
    got = lax.all_to_all(parcel, "blk", 0, 0, tiled=True)
    steps = 4
    chunk = devices // steps

    def kernel(got_ref, out_ref):
        step = pl.program_id(0)
        pairs_all = got_ref[:, :rows, :].reshape(devices * rows, 2 * HEAD)
        asked_now = got_ref[pl.ds(step * chunk, chunk), rows:, :].reshape(chunk * part, 2 * HEAD)
        scores = lax.dot_general(
            asked_now, pairs_all, (((1,), (1,)), ((), ())), preferred_element_type=jnp.float32
        ) * scale
        highest = jnp.max(scores, axis=-1, keepdims=True)
        expo = jnp.exp(scores - highest)
        denom = jnp.sum(expo, axis=-1, keepdims=True)
        totals = jnp.dot(expo.astype(jnp.bfloat16), pairs_all, preferred_element_type=jnp.float32)
        out_ref[...] = (totals[:, HEAD:] / denom).astype(jnp.bfloat16).reshape(chunk, part, HEAD)

    queries_total = devices * part
    keys_total = devices * rows
    mixed = pl.pallas_call(
        kernel,
        grid=(steps,),
        in_specs=[pl.BlockSpec(got.shape, lambda i: (0, 0, 0))],
        out_specs=pl.BlockSpec((chunk, part, HEAD), lambda i: (i, 0, 0)),
        out_shape=jax.ShapeDtypeStruct((devices, part, HEAD), jnp.bfloat16),
        compiler_params=pltpu.CompilerParams(vmem_limit_bytes=48 * 1024 * 1024),
        cost_estimate=pl.CostEstimate(
            flops=4 * queries_total * keys_total * 2 * HEAD,
            transcendentals=queries_total * keys_total,
            bytes_accessed=got.size * 2 + queries_total * HEAD * 2,
        ),
    )(got)
    back = lax.all_to_all(mixed, "blk", 0, 0, tiled=True)
    back = jnp.transpose(back.reshape(HEADS, groups, part, HEAD), (1, 2, 0, 3))
    return back.reshape(rows, HEADS * HEAD)


def block(
    residual,
    queries,
    key_rows,
    value_rows,
    w_out,
    expert_ids,
    route_gates,
    cotangent,
    w_gate,
    w_up,
    w_down,
):
    row_count = queries.shape[1]
    route_experts = expert_ids[0].reshape(-1)
    gates = route_gates[0].reshape(-1)
    onehot = (route_experts[:, None] == jnp.arange(EXPERTS, dtype=jnp.int32)[None, :]).astype(
        jnp.int32
    )
    before = jnp.cumsum(onehot, axis=0) - onehot
    position = jnp.sum(before * onehot, axis=1)
    slot_index = route_experts * CAP + position
    grad_flat = cotangent[0].astype(jnp.float32)
    route_cots = (gates[:, None] * jnp.repeat(grad_flat, TOP, axis=0)).astype(jnp.bfloat16)
    half = CAP // PIECES
    slot_ids = jnp.arange(EXPERTS * CAP, dtype=jnp.int32).reshape(EXPERTS * PIECES, half)
    placing = (slot_ids[:, :, None] == slot_index[None, None, :]).astype(jnp.bfloat16)
    attended = attend_heads(queries[0], key_rows[0], value_rows[0])
    stream = residual[0].astype(jnp.float32) + jnp.dot(
        attended, w_out, preferred_element_type=jnp.float32
    )
    radius = jnp.sqrt(jnp.mean(stream * stream, axis=-1, keepdims=True) + 1e-06)
    unit = stream / radius
    normed = unit.astype(jnp.bfloat16)
    route_rows = jnp.concatenate([jnp.repeat(normed, TOP, axis=0), route_cots], axis=1)
    in_slots = jnp.einsum(
        "jcr,rw->jcw", placing, route_rows, preferred_element_type=jnp.float32
    ).astype(jnp.bfloat16)
    both_own, both_other = spread(in_slots)
    in_own, cot_own = both_own[..., :D], both_own[..., D:]
    in_other, cot_other = both_other[..., :D], both_other[..., D:]
    mats = (w_gate[0], w_up[0], w_down[0])
    own, gate_a, up_a, down_a = piece_pass(in_own, cot_own, *mats)
    other, gate_b, up_b, down_b = piece_pass(in_other, cot_other, *mats)
    theirs = lax.ppermute(other, "blk", partner_pairs())
    summed = (own.astype(jnp.float32) + theirs.astype(jnp.float32)).astype(jnp.bfloat16)
    back = to_anchor(summed)
    picking = (slot_index[:, None, None] == slot_ids[None, :, :]).astype(jnp.bfloat16)
    picked = jnp.einsum("rjc,jcw->rw", picking, back, preferred_element_type=jnp.float32)
    route_out = picked[:, :D]
    route_grad = picked[:, D:]
    grad_gate = (gate_a + gate_b).astype(jnp.bfloat16)[None]
    grad_up = (up_a + up_b).astype(jnp.bfloat16)[None]
    grad_down = (down_a + down_b).astype(jnp.bfloat16)[None]
    moe = jnp.sum((gates[:, None] * route_out).reshape(row_count, TOP, D), axis=1)
    block_out = (stream + moe).astype(jnp.bfloat16)[None]
    grad_unit = jnp.sum(route_grad.reshape(row_count, TOP, D), axis=1)
    grad_stream = (
        grad_flat + (grad_unit - unit * jnp.mean(grad_unit * unit, axis=-1, keepdims=True)) / radius
    )
    return (block_out, grad_stream.astype(jnp.bfloat16)[None], grad_gate, grad_up, grad_down)


def solution(mesh):
    return jax.shard_map(
        block,
        mesh=mesh,
        in_specs=(
            P("table", "blk", None),
            P("table", "blk", None),
            P("table", "blk", None),
            P("table", "blk", None),
            P(),
            P("table", "blk", None),
            P("table", "blk", None),
            P("table", "blk", None),
            P(("table", "blk"), None, None),
            P(("table", "blk"), None, None),
            P(("table", "blk"), None, None),
        ),
        out_specs=(
            P("table", "blk", None),
            P("table", "blk", None),
            P(("table", "blk"), None, None),
            P(("table", "blk"), None, None),
            P(("table", "blk"), None, None),
        ),
        check_vma=False,
    )
```

```python
import math

import jax
import jax.numpy as jnp
from jax import lax
from jax.experimental import pallas as pl
from jax.experimental.pallas import tpu as pltpu
from jax.sharding import PartitionSpec as P


D = 512
HEADS = 8
HEAD = 64
EXPERTS = 64
TOP = 2
PIECES = 2
CAP = 12


def silu_grad(pre):
    sig = jax.nn.sigmoid(pre)
    return sig * (1.0 + pre * (1.0 - sig))


def to_experts(buffer):
    return lax.all_to_all(buffer, ("table", "blk"), split_axis=0, concat_axis=0, tiled=True)


def to_anchor(buffer):
    return lax.all_to_all(buffer, ("table", "blk"), split_axis=0, concat_axis=0, tiled=True)


def partner_pairs():
    devices = lax.psum(1, "blk")
    return [(b, b ^ 1) for b in range(devices)]


def spread(slots):
    got = to_experts(slots)
    other = lax.ppermute(got, "blk", partner_pairs())
    return got, other


def piece_pass(inputs, cots, gate_mat, up_mat, down_mat):
    pre_gate = jnp.einsum("scd,df->scf", inputs, gate_mat, preferred_element_type=jnp.float32)
    pre_up = jnp.einsum("scd,df->scf", inputs, up_mat, preferred_element_type=jnp.float32)
    activated = jax.nn.silu(pre_gate)
    hidden = (activated * pre_up).astype(jnp.bfloat16)
    output = jnp.einsum(
        "scf,fd->scd", hidden, down_mat, preferred_element_type=jnp.float32
    ).astype(jnp.bfloat16)
    grad_hidden = jnp.einsum("scd,fd->scf", cots, down_mat, preferred_element_type=jnp.float32)
    grad_pre_gate = (grad_hidden * pre_up * silu_grad(pre_gate)).astype(jnp.bfloat16)
    grad_pre_up = (grad_hidden * activated).astype(jnp.bfloat16)
    grad_inputs = (
        jnp.einsum("scf,df->scd", grad_pre_gate, gate_mat, preferred_element_type=jnp.float32)
        + jnp.einsum("scf,df->scd", grad_pre_up, up_mat, preferred_element_type=jnp.float32)
    ).astype(jnp.bfloat16)
    grad_down = jnp.einsum("scf,scd->fd", hidden, cots, preferred_element_type=jnp.float32)
    grad_gate = jnp.einsum("scd,scf->df", inputs, grad_pre_gate, preferred_element_type=jnp.float32)
    grad_up = jnp.einsum("scd,scf->df", inputs, grad_pre_up, preferred_element_type=jnp.float32)
    return (jnp.concatenate([output, grad_inputs], axis=-1), grad_gate, grad_up, grad_down)


def attend_heads(query_rows, key_rows, value_rows):
    rows = query_rows.shape[0]
    devices = lax.psum(1, "blk")
    groups = devices // HEADS
    part = rows // groups
    kept = rows // 2
    scale = 1.0 / math.sqrt(HEAD)

    def by_head(block):
        return jnp.transpose(block.reshape(rows, HEADS, HEAD), (1, 0, 2))

    pairs = jnp.concatenate([by_head(key_rows), by_head(value_rows)], axis=-1)
    pairs = pairs.reshape(HEADS, 1, 2, kept, 2 * HEAD)
    pairs = jnp.broadcast_to(pairs, (HEADS, groups // 2, 2, kept, 2 * HEAD))
    pairs = pairs.reshape(devices, kept, 2 * HEAD)
    asked = jnp.transpose(query_rows.reshape(groups, part, HEADS, HEAD), (2, 0, 1, 3))
    asked = asked.reshape(devices, part, HEAD)
    asked = jnp.concatenate([asked, jnp.zeros_like(asked)], axis=-1)
    parcel = jnp.concatenate([pairs, asked], axis=1)
    got = lax.all_to_all(parcel, "blk", 0, 0, tiled=True)
    other = lax.ppermute(got[:, :kept, :], "blk", partner_pairs())
    steps = 4
    chunk = devices // steps

    def kernel(got_ref, other_ref, out_ref):
        step = pl.program_id(0)
        near = got_ref[:, :kept, :].reshape(devices * kept, 2 * HEAD)
        far = other_ref[...].reshape(devices * kept, 2 * HEAD)
        asked_now = got_ref[pl.ds(step * chunk, chunk), kept:, :].reshape(chunk * part, 2 * HEAD)
        dims = (((1,), (1,)), ((), ()))
        near_scores = lax.dot_general(asked_now, near, dims, preferred_element_type=jnp.float32) * scale
        far_scores = lax.dot_general(asked_now, far, dims, preferred_element_type=jnp.float32) * scale
        highest = jnp.maximum(
            jnp.max(near_scores, axis=-1, keepdims=True), jnp.max(far_scores, axis=-1, keepdims=True)
        )
        near_expo = jnp.exp(near_scores - highest)
        far_expo = jnp.exp(far_scores - highest)
        denom = jnp.sum(near_expo, axis=-1, keepdims=True) + jnp.sum(far_expo, axis=-1, keepdims=True)
        totals = jnp.dot(
            near_expo.astype(jnp.bfloat16), near, preferred_element_type=jnp.float32
        ) + jnp.dot(far_expo.astype(jnp.bfloat16), far, preferred_element_type=jnp.float32)
        out_ref[...] = (totals[:, HEAD:] / denom).astype(jnp.bfloat16).reshape(chunk, part, HEAD)

    queries_total = devices * part
    keys_total = devices * rows
    mixed = pl.pallas_call(
        kernel,
        grid=(steps,),
        in_specs=[
            pl.BlockSpec(got.shape, lambda i: (0, 0, 0)),
            pl.BlockSpec(other.shape, lambda i: (0, 0, 0)),
        ],
        out_specs=pl.BlockSpec((chunk, part, HEAD), lambda i: (i, 0, 0)),
        out_shape=jax.ShapeDtypeStruct((devices, part, HEAD), jnp.bfloat16),
        compiler_params=pltpu.CompilerParams(vmem_limit_bytes=48 * 1024 * 1024),
        cost_estimate=pl.CostEstimate(
            flops=4 * queries_total * keys_total * 2 * HEAD,
            transcendentals=queries_total * keys_total,
            bytes_accessed=(got.size + other.size) * 2 + queries_total * HEAD * 2,
        ),
    )(got, other)
    back = lax.all_to_all(mixed, "blk", 0, 0, tiled=True)
    back = jnp.transpose(back.reshape(HEADS, groups, part, HEAD), (1, 2, 0, 3))
    return back.reshape(rows, HEADS * HEAD)


def block(
    residual,
    queries,
    key_rows,
    value_rows,
    w_out,
    expert_ids,
    route_gates,
    cotangent,
    w_gate,
    w_up,
    w_down,
):
    row_count = queries.shape[1]
    route_experts = expert_ids[0].reshape(-1)
    gates = route_gates[0].reshape(-1)
    onehot = (route_experts[:, None] == jnp.arange(EXPERTS, dtype=jnp.int32)[None, :]).astype(
        jnp.int32
    )
    before = jnp.cumsum(onehot, axis=0) - onehot
    position = jnp.sum(before * onehot, axis=1)
    slot_index = route_experts * CAP + position
    grad_flat = cotangent[0].astype(jnp.float32)
    route_cots = (gates[:, None] * jnp.repeat(grad_flat, TOP, axis=0)).astype(jnp.bfloat16)
    half = CAP // PIECES
    slot_ids = jnp.arange(EXPERTS * CAP, dtype=jnp.int32).reshape(EXPERTS * PIECES, half)
    placing = (slot_ids[:, :, None] == slot_index[None, None, :]).astype(jnp.bfloat16)
    attended = attend_heads(queries[0], key_rows[0], value_rows[0])
    stream = residual[0].astype(jnp.float32) + jnp.dot(
        attended, w_out, preferred_element_type=jnp.float32
    )
    radius = jnp.sqrt(jnp.mean(stream * stream, axis=-1, keepdims=True) + 1e-06)
    unit = stream / radius
    normed = unit.astype(jnp.bfloat16)
    route_rows = jnp.concatenate([jnp.repeat(normed, TOP, axis=0), route_cots], axis=1)
    in_slots = jnp.einsum(
        "jcr,rw->jcw", placing, route_rows, preferred_element_type=jnp.float32
    ).astype(jnp.bfloat16)
    both_own, both_other = spread(in_slots)
    in_own, cot_own = both_own[..., :D], both_own[..., D:]
    in_other, cot_other = both_other[..., :D], both_other[..., D:]
    mats = (w_gate[0], w_up[0], w_down[0])
    own, gate_a, up_a, down_a = piece_pass(in_own, cot_own, *mats)
    other, gate_b, up_b, down_b = piece_pass(in_other, cot_other, *mats)
    theirs = lax.ppermute(other, "blk", partner_pairs())
    summed = (own.astype(jnp.float32) + theirs.astype(jnp.float32)).astype(jnp.bfloat16)
    back = to_anchor(summed)
    picking = (slot_index[:, None, None] == slot_ids[None, :, :]).astype(jnp.bfloat16)
    picked = jnp.einsum("rjc,jcw->rw", picking, back, preferred_element_type=jnp.float32)
    route_out = picked[:, :D]
    route_grad = picked[:, D:]
    grad_gate = (gate_a + gate_b).astype(jnp.bfloat16)[None]
    grad_up = (up_a + up_b).astype(jnp.bfloat16)[None]
    grad_down = (down_a + down_b).astype(jnp.bfloat16)[None]
    moe = jnp.sum((gates[:, None] * route_out).reshape(row_count, TOP, D), axis=1)
    block_out = (stream + moe).astype(jnp.bfloat16)[None]
    grad_unit = jnp.sum(route_grad.reshape(row_count, TOP, D), axis=1)
    grad_stream = (
        grad_flat + (grad_unit - unit * jnp.mean(grad_unit * unit, axis=-1, keepdims=True)) / radius
    )
    return (block_out, grad_stream.astype(jnp.bfloat16)[None], grad_gate, grad_up, grad_down)


def solution(mesh):
    return jax.shard_map(
        block,
        mesh=mesh,
        in_specs=(
            P("table", "blk", None),
            P("table", "blk", None),
            P("table", "blk", None),
            P("table", "blk", None),
            P(),
            P("table", "blk", None),
            P("table", "blk", None),
            P("table", "blk", None),
            P(("table", "blk"), None, None),
            P(("table", "blk"), None, None),
            P(("table", "blk"), None, None),
        ),
        out_specs=(
            P("table", "blk", None),
            P("table", "blk", None),
            P(("table", "blk"), None, None),
            P(("table", "blk"), None, None),
            P(("table", "blk"), None, None),
        ),
        check_vma=False,
    )
```

```python
import math

import jax
import jax.numpy as jnp
from jax import lax
from jax.experimental import pallas as pl
from jax.experimental.pallas import tpu as pltpu
from jax.sharding import PartitionSpec as P


D = 512
HEADS = 8
HEAD = 64
EXPERTS = 64
TOP = 2
PIECES = 2
CAP = 12


def silu_grad(pre):
    sig = jax.nn.sigmoid(pre)
    return sig * (1.0 + pre * (1.0 - sig))


def to_experts(buffer):
    return lax.all_to_all(buffer, ("table", "blk"), split_axis=0, concat_axis=0, tiled=True)


def to_anchor(buffer):
    return lax.all_to_all(buffer, ("table", "blk"), split_axis=0, concat_axis=0, tiled=True)


def partner_pairs():
    devices = lax.psum(1, "blk")
    return [(b, b ^ 1) for b in range(devices)]


def spread(slots):
    got = to_experts(slots)
    other = lax.ppermute(got, "blk", partner_pairs())
    return got, other


def piece_pass(inputs, cots, gate_mat, up_mat, down_mat):
    pre_gate = jnp.einsum("scd,df->scf", inputs, gate_mat, preferred_element_type=jnp.float32)
    pre_up = jnp.einsum("scd,df->scf", inputs, up_mat, preferred_element_type=jnp.float32)
    activated = jax.nn.silu(pre_gate)
    hidden = (activated * pre_up).astype(jnp.bfloat16)
    output = jnp.einsum(
        "scf,fd->scd", hidden, down_mat, preferred_element_type=jnp.float32
    ).astype(jnp.bfloat16)
    grad_hidden = jnp.einsum("scd,fd->scf", cots, down_mat, preferred_element_type=jnp.float32)
    grad_pre_gate = (grad_hidden * pre_up * silu_grad(pre_gate)).astype(jnp.bfloat16)
    grad_pre_up = (grad_hidden * activated).astype(jnp.bfloat16)
    grad_inputs = (
        jnp.einsum("scf,df->scd", grad_pre_gate, gate_mat, preferred_element_type=jnp.float32)
        + jnp.einsum("scf,df->scd", grad_pre_up, up_mat, preferred_element_type=jnp.float32)
    ).astype(jnp.bfloat16)
    grad_down = jnp.einsum("scf,scd->fd", hidden, cots, preferred_element_type=jnp.float32)
    grad_gate = jnp.einsum("scd,scf->df", inputs, grad_pre_gate, preferred_element_type=jnp.float32)
    grad_up = jnp.einsum("scd,scf->df", inputs, grad_pre_up, preferred_element_type=jnp.float32)
    return (jnp.concatenate([output, grad_inputs], axis=-1), grad_gate, grad_up, grad_down)


def attend_heads(query_rows, key_rows, value_rows):
    rows = query_rows.shape[0]
    devices = lax.psum(1, "blk")
    groups = devices // HEADS
    part = rows // groups
    kept = rows // 2
    scale = 1.0 / math.sqrt(HEAD)

    def by_head(block):
        return jnp.transpose(block.reshape(rows, HEADS, HEAD), (1, 0, 2))

    pairs = jnp.concatenate([by_head(key_rows), by_head(value_rows)], axis=-1)
    pairs = pairs.reshape(HEADS, 1, 2, kept, 2 * HEAD)
    pairs = jnp.broadcast_to(pairs, (HEADS, groups // 2, 2, kept, 2 * HEAD))
    pairs = pairs.reshape(devices, kept, 2 * HEAD)
    asked = jnp.transpose(query_rows.reshape(groups, part, HEADS, HEAD), (2, 0, 1, 3))
    asked = asked.reshape(devices, part, HEAD)
    asked = jnp.concatenate([asked, jnp.zeros_like(asked)], axis=-1)
    parcel = jnp.concatenate([pairs, asked], axis=1)
    got = lax.all_to_all(parcel, "blk", 0, 0, tiled=True)
    other = lax.ppermute(got[:, :kept, :], "blk", partner_pairs())
    steps = 4
    chunk = devices // steps

    def kernel(got_ref, other_ref, out_ref):
        step = pl.program_id(0)
        near = got_ref[:, :kept, :].reshape(devices * kept, 2 * HEAD)
        far = other_ref[...].reshape(devices * kept, 2 * HEAD)
        asked_now = got_ref[pl.ds(step * chunk, chunk), kept:, :].reshape(chunk * part, 2 * HEAD)
        dims = (((1,), (1,)), ((), ()))
        near_scores = lax.dot_general(asked_now, near, dims, preferred_element_type=jnp.float32) * scale
        far_scores = lax.dot_general(asked_now, far, dims, preferred_element_type=jnp.float32) * scale
        highest = jnp.maximum(
            jnp.max(near_scores, axis=-1, keepdims=True), jnp.max(far_scores, axis=-1, keepdims=True)
        )
        near_expo = jnp.exp(near_scores - highest)
        far_expo = jnp.exp(far_scores - highest)
        denom = jnp.sum(near_expo, axis=-1, keepdims=True) + jnp.sum(far_expo, axis=-1, keepdims=True)
        totals = jnp.dot(
            near_expo.astype(jnp.bfloat16), near, preferred_element_type=jnp.float32
        ) + jnp.dot(far_expo.astype(jnp.bfloat16), far, preferred_element_type=jnp.float32)
        out_ref[...] = (totals[:, HEAD:] / denom).astype(jnp.bfloat16).reshape(chunk, part, HEAD)

    queries_total = devices * part
    keys_total = devices * rows
    mixed = pl.pallas_call(
        kernel,
        grid=(steps,),
        in_specs=[
            pl.BlockSpec(got.shape, lambda i: (0, 0, 0)),
            pl.BlockSpec(other.shape, lambda i: (0, 0, 0)),
        ],
        out_specs=pl.BlockSpec((chunk, part, HEAD), lambda i: (i, 0, 0)),
        out_shape=jax.ShapeDtypeStruct((devices, part, HEAD), jnp.bfloat16),
        compiler_params=pltpu.CompilerParams(vmem_limit_bytes=48 * 1024 * 1024),
        cost_estimate=pl.CostEstimate(
            flops=4 * queries_total * keys_total * 2 * HEAD,
            transcendentals=queries_total * keys_total,
            bytes_accessed=(got.size + other.size) * 2 + queries_total * HEAD * 2,
        ),
    )(got, other)
    back = lax.all_to_all(mixed, "blk", 0, 0, tiled=True)
    back = jnp.transpose(back.reshape(HEADS, groups, part, HEAD), (1, 2, 0, 3))
    return back.reshape(rows, HEADS * HEAD)


def block(
    residual,
    queries,
    key_rows,
    value_rows,
    w_out,
    expert_ids,
    route_gates,
    cotangent,
    w_gate,
    w_up,
    w_down,
):
    row_count = queries.shape[1]
    route_experts = expert_ids[0].reshape(-1)
    gates = route_gates[0].reshape(-1)
    onehot = (route_experts[:, None] == jnp.arange(EXPERTS, dtype=jnp.int32)[None, :]).astype(
        jnp.int32
    )
    before = jnp.cumsum(onehot, axis=0) - onehot
    position = jnp.sum(before * onehot, axis=1)
    slot_index = route_experts * CAP + position
    grad_flat = cotangent[0].astype(jnp.float32)
    route_cots = (gates[:, None] * jnp.repeat(grad_flat, TOP, axis=0)).astype(jnp.bfloat16)
    half = CAP // PIECES
    slot_ids = jnp.arange(EXPERTS * CAP, dtype=jnp.int32).reshape(EXPERTS * PIECES, half)
    placing = (slot_ids[:, :, None] == slot_index[None, None, :]).astype(jnp.bfloat16)
    attended = attend_heads(queries[0], key_rows[0], value_rows[0])
    stream = residual[0].astype(jnp.float32) + jnp.dot(
        attended, w_out, preferred_element_type=jnp.float32
    )
    radius = jnp.sqrt(jnp.mean(stream * stream, axis=-1, keepdims=True) + 1e-06)
    unit = stream / radius
    normed = unit.astype(jnp.bfloat16)
    route_rows = jnp.concatenate([jnp.repeat(normed, TOP, axis=0), route_cots], axis=1)
    in_slots = jnp.einsum(
        "jcr,rw->jcw", placing, route_rows, preferred_element_type=jnp.float32
    ).astype(jnp.bfloat16)
    both_own, both_other = spread(in_slots)
    both = jnp.concatenate([both_own, both_other], axis=0)
    mats = (w_gate[0], w_up[0], w_down[0])
    done, gate_sum, up_sum, down_sum = piece_pass(both[..., :D], both[..., D:], *mats)
    own, other = done[: both_own.shape[0]], done[both_own.shape[0] :]
    theirs = lax.ppermute(other, "blk", partner_pairs())
    summed = (own.astype(jnp.float32) + theirs.astype(jnp.float32)).astype(jnp.bfloat16)
    back = to_anchor(summed)
    picking = (slot_index[:, None, None] == slot_ids[None, :, :]).astype(jnp.bfloat16)
    picked = jnp.einsum("rjc,jcw->rw", picking, back, preferred_element_type=jnp.float32)
    route_out = picked[:, :D]
    route_grad = picked[:, D:]
    grad_gate = gate_sum.astype(jnp.bfloat16)[None]
    grad_up = up_sum.astype(jnp.bfloat16)[None]
    grad_down = down_sum.astype(jnp.bfloat16)[None]
    moe = jnp.sum((gates[:, None] * route_out).reshape(row_count, TOP, D), axis=1)
    block_out = (stream + moe).astype(jnp.bfloat16)[None]
    grad_unit = jnp.sum(route_grad.reshape(row_count, TOP, D), axis=1)
    grad_stream = (
        grad_flat + (grad_unit - unit * jnp.mean(grad_unit * unit, axis=-1, keepdims=True)) / radius
    )
    return (block_out, grad_stream.astype(jnp.bfloat16)[None], grad_gate, grad_up, grad_down)


def solution(mesh):
    return jax.shard_map(
        block,
        mesh=mesh,
        in_specs=(
            P("table", "blk", None),
            P("table", "blk", None),
            P("table", "blk", None),
            P("table", "blk", None),
            P(),
            P("table", "blk", None),
            P("table", "blk", None),
            P("table", "blk", None),
            P(("table", "blk"), None, None),
            P(("table", "blk"), None, None),
            P(("table", "blk"), None, None),
        ),
        out_specs=(
            P("table", "blk", None),
            P("table", "blk", None),
            P(("table", "blk"), None, None),
            P(("table", "blk"), None, None),
            P(("table", "blk"), None, None),
        ),
        check_vma=False,
    )
```

```python
import math

import jax
import jax.numpy as jnp
from jax import lax
from jax.experimental import pallas as pl
from jax.experimental.pallas import tpu as pltpu
from jax.sharding import PartitionSpec as P


D = 512
HEADS = 8
HEAD = 64
EXPERTS = 64
TOP = 2
PIECES = 2
CAP = 12


def silu_grad(pre):
    sig = jax.nn.sigmoid(pre)
    return sig * (1.0 + pre * (1.0 - sig))


def to_experts(buffer):
    return lax.all_to_all(buffer, ("table", "blk"), split_axis=0, concat_axis=0, tiled=True)


def to_anchor(buffer):
    return lax.all_to_all(buffer, ("table", "blk"), split_axis=0, concat_axis=0, tiled=True)


def partner_pairs():
    devices = lax.psum(1, "blk")
    return [(b, b ^ 1) for b in range(devices)]


def spread(slots):
    got = to_experts(slots)
    other = lax.ppermute(got, "blk", partner_pairs())
    return got, other


def piece_pass(inputs, cots, gate_mat, up_mat, down_mat):
    pre_gate = jnp.einsum("scd,df->scf", inputs, gate_mat, preferred_element_type=jnp.float32)
    pre_up = jnp.einsum("scd,df->scf", inputs, up_mat, preferred_element_type=jnp.float32)
    activated = jax.nn.silu(pre_gate)
    hidden = (activated * pre_up).astype(jnp.bfloat16)
    output = jnp.einsum(
        "scf,fd->scd", hidden, down_mat, preferred_element_type=jnp.float32
    ).astype(jnp.bfloat16)
    grad_hidden = jnp.einsum("scd,fd->scf", cots, down_mat, preferred_element_type=jnp.float32)
    grad_pre_gate = (grad_hidden * pre_up * silu_grad(pre_gate)).astype(jnp.bfloat16)
    grad_pre_up = (grad_hidden * activated).astype(jnp.bfloat16)
    grad_inputs = (
        jnp.einsum("scf,df->scd", grad_pre_gate, gate_mat, preferred_element_type=jnp.float32)
        + jnp.einsum("scf,df->scd", grad_pre_up, up_mat, preferred_element_type=jnp.float32)
    ).astype(jnp.bfloat16)
    grad_down = jnp.einsum("scf,scd->fd", hidden, cots, preferred_element_type=jnp.float32)
    grad_gate = jnp.einsum("scd,scf->df", inputs, grad_pre_gate, preferred_element_type=jnp.float32)
    grad_up = jnp.einsum("scd,scf->df", inputs, grad_pre_up, preferred_element_type=jnp.float32)
    return (jnp.concatenate([output, grad_inputs], axis=-1), grad_gate, grad_up, grad_down)


def attend_heads(query_rows, key_rows, value_rows):
    rows = query_rows.shape[0]
    devices = lax.psum(1, "blk")
    groups = devices // HEADS
    part = rows // groups
    kept = rows // 2
    scale = 1.0 / math.sqrt(HEAD)

    def by_head(block):
        return jnp.transpose(block.reshape(rows, HEADS, HEAD), (1, 0, 2))

    pairs = jnp.concatenate([by_head(key_rows), by_head(value_rows)], axis=-1)
    pairs = pairs.reshape(HEADS, 1, 2, kept, 2 * HEAD)
    pairs = jnp.broadcast_to(pairs, (HEADS, groups // 2, 2, kept, 2 * HEAD))
    pairs = pairs.reshape(devices, kept, 2 * HEAD)
    asked = jnp.transpose(query_rows.reshape(groups, part, HEADS, HEAD), (2, 0, 1, 3))
    asked = asked.reshape(devices, part, HEAD)
    asked = jnp.concatenate([asked, jnp.zeros_like(asked)], axis=-1)
    parcel = jnp.concatenate([pairs, asked], axis=1)
    got = lax.all_to_all(parcel, "blk", 0, 0, tiled=True)
    other = lax.ppermute(got[:, :kept, :], "blk", partner_pairs())
    steps = 4
    chunk = devices // steps

    def kernel(got_ref, other_ref, out_ref):
        step = pl.program_id(0)
        near = got_ref[:, :kept, :].reshape(devices * kept, 2 * HEAD)
        far = other_ref[...].reshape(devices * kept, 2 * HEAD)
        asked_now = got_ref[pl.ds(step * chunk, chunk), kept:, :].reshape(chunk * part, 2 * HEAD)
        dims = (((1,), (1,)), ((), ()))
        near_scores = lax.dot_general(asked_now, near, dims, preferred_element_type=jnp.float32) * scale
        far_scores = lax.dot_general(asked_now, far, dims, preferred_element_type=jnp.float32) * scale
        highest = jnp.maximum(
            jnp.max(near_scores, axis=-1, keepdims=True), jnp.max(far_scores, axis=-1, keepdims=True)
        )
        near_expo = jnp.exp(near_scores - highest)
        far_expo = jnp.exp(far_scores - highest)
        denom = jnp.sum(near_expo, axis=-1, keepdims=True) + jnp.sum(far_expo, axis=-1, keepdims=True)
        totals = jnp.dot(
            near_expo.astype(jnp.bfloat16), near, preferred_element_type=jnp.float32
        ) + jnp.dot(far_expo.astype(jnp.bfloat16), far, preferred_element_type=jnp.float32)
        out_ref[...] = (totals[:, HEAD:] / denom).astype(jnp.bfloat16).reshape(chunk, part, HEAD)

    queries_total = devices * part
    keys_total = devices * rows
    mixed = pl.pallas_call(
        kernel,
        grid=(steps,),
        in_specs=[
            pl.BlockSpec(got.shape, lambda i: (0, 0, 0)),
            pl.BlockSpec(other.shape, lambda i: (0, 0, 0)),
        ],
        out_specs=pl.BlockSpec((chunk, part, HEAD), lambda i: (i, 0, 0)),
        out_shape=jax.ShapeDtypeStruct((devices, part, HEAD), jnp.bfloat16),
        compiler_params=pltpu.CompilerParams(vmem_limit_bytes=48 * 1024 * 1024),
        cost_estimate=pl.CostEstimate(
            flops=4 * queries_total * keys_total * 2 * HEAD,
            transcendentals=queries_total * keys_total,
            bytes_accessed=(got.size + other.size) * 2 + queries_total * HEAD * 2,
        ),
    )(got, other)
    back = lax.all_to_all(mixed, "blk", 0, 0, tiled=True)
    back = jnp.transpose(back.reshape(HEADS, groups, part, HEAD), (1, 2, 0, 3))
    return back.reshape(rows, HEADS * HEAD)


def block(
    residual,
    queries,
    key_rows,
    value_rows,
    w_out,
    expert_ids,
    route_gates,
    cotangent,
    w_gate,
    w_up,
    w_down,
):
    row_count = queries.shape[1]
    route_experts = expert_ids[0].reshape(-1)
    gates = route_gates[0].reshape(-1)
    onehot = (route_experts[:, None] == jnp.arange(EXPERTS, dtype=jnp.int32)[None, :]).astype(
        jnp.int32
    )
    before = jnp.cumsum(onehot, axis=0) - onehot
    position = jnp.sum(before * onehot, axis=1)
    slot_index = route_experts * CAP + position
    grad_flat = cotangent[0].astype(jnp.float32)
    route_cots = (gates[:, None] * jnp.repeat(grad_flat, TOP, axis=0)).astype(jnp.bfloat16)
    half = CAP // PIECES
    slot_ids = jnp.arange(EXPERTS * CAP, dtype=jnp.int32).reshape(EXPERTS * PIECES, half)
    placing = (slot_ids[:, :, None] == slot_index[None, None, :]).astype(jnp.bfloat16)
    attended = attend_heads(queries[0], key_rows[0], value_rows[0])
    stream = residual[0].astype(jnp.float32) + jnp.dot(
        attended, w_out, preferred_element_type=jnp.float32
    )
    radius = jnp.sqrt(jnp.mean(stream * stream, axis=-1, keepdims=True) + 1e-06)
    unit = stream / radius
    normed = unit.astype(jnp.bfloat16)
    route_rows = jnp.concatenate([jnp.repeat(normed, TOP, axis=0), route_cots], axis=1)
    in_slots = jnp.einsum(
        "jcr,rw->jcw", placing, route_rows, preferred_element_type=jnp.float32
    ).astype(jnp.bfloat16)
    both_own, both_other = spread(in_slots)
    in_own, cot_own = both_own[..., :D], both_own[..., D:]
    in_other, cot_other = both_other[..., :D], both_other[..., D:]
    mats = (w_gate[0], w_up[0], w_down[0])
    own, gate_a, up_a, down_a = piece_pass(in_own, cot_own, *mats)
    other, gate_b, up_b, down_b = piece_pass(in_other, cot_other, *mats)
    theirs = lax.ppermute(other, "blk", partner_pairs())
    summed = (own.astype(jnp.float32) + theirs.astype(jnp.float32)).astype(jnp.bfloat16)
    back = to_anchor(summed)
    picking = (slot_index[:, None] == slot_ids.reshape(1, -1)).astype(jnp.bfloat16)
    picked = jnp.dot(
        picking, back.reshape(EXPERTS * CAP, 2 * D), preferred_element_type=jnp.float32
    )
    route_out = picked[:, :D]
    route_grad = picked[:, D:]
    grad_gate = (gate_a + gate_b).astype(jnp.bfloat16)[None]
    grad_up = (up_a + up_b).astype(jnp.bfloat16)[None]
    grad_down = (down_a + down_b).astype(jnp.bfloat16)[None]
    moe = jnp.sum((gates[:, None] * route_out).reshape(row_count, TOP, D), axis=1)
    block_out = (stream + moe).astype(jnp.bfloat16)[None]
    grad_unit = jnp.sum(route_grad.reshape(row_count, TOP, D), axis=1)
    grad_stream = (
        grad_flat + (grad_unit - unit * jnp.mean(grad_unit * unit, axis=-1, keepdims=True)) / radius
    )
    return (block_out, grad_stream.astype(jnp.bfloat16)[None], grad_gate, grad_up, grad_down)


def solution(mesh):
    return jax.shard_map(
        block,
        mesh=mesh,
        in_specs=(
            P("table", "blk", None),
            P("table", "blk", None),
            P("table", "blk", None),
            P("table", "blk", None),
            P(),
            P("table", "blk", None),
            P("table", "blk", None),
            P("table", "blk", None),
            P(("table", "blk"), None, None),
            P(("table", "blk"), None, None),
            P(("table", "blk"), None, None),
        ),
        out_specs=(
            P("table", "blk", None),
            P("table", "blk", None),
            P(("table", "blk"), None, None),
            P(("table", "blk"), None, None),
            P(("table", "blk"), None, None),
        ),
        check_vma=False,
    )
```

```python
import math

import jax
import jax.numpy as jnp
from jax import lax
from jax.experimental import pallas as pl
from jax.experimental.pallas import tpu as pltpu
from jax.sharding import PartitionSpec as P


D = 512
HEADS = 8
HEAD = 64
EXPERTS = 64
TOP = 2
PIECES = 2
CAP = 12


def silu_grad(pre):
    sig = jax.nn.sigmoid(pre)
    return sig * (1.0 + pre * (1.0 - sig))


def to_experts(buffer):
    return lax.all_to_all(buffer, ("table", "blk"), split_axis=0, concat_axis=0, tiled=True)


def to_anchor(buffer):
    return lax.all_to_all(buffer, ("table", "blk"), split_axis=0, concat_axis=0, tiled=True)


def partner_pairs():
    devices = lax.psum(1, "blk")
    return [(b, b ^ 1) for b in range(devices)]


def spread(slots):
    got = to_experts(slots)
    other = lax.ppermute(got, "blk", partner_pairs())
    return got, other


def piece_pass(inputs, cots, gate_mat, up_mat, down_mat):
    pre_gate = jnp.einsum("scd,df->scf", inputs, gate_mat, preferred_element_type=jnp.float32)
    pre_up = jnp.einsum("scd,df->scf", inputs, up_mat, preferred_element_type=jnp.float32)
    activated = jax.nn.silu(pre_gate)
    hidden = (activated * pre_up).astype(jnp.bfloat16)
    output = jnp.einsum(
        "scf,fd->scd", hidden, down_mat, preferred_element_type=jnp.float32
    ).astype(jnp.bfloat16)
    grad_hidden = jnp.einsum("scd,fd->scf", cots, down_mat, preferred_element_type=jnp.float32)
    grad_pre_gate = (grad_hidden * pre_up * silu_grad(pre_gate)).astype(jnp.bfloat16)
    grad_pre_up = (grad_hidden * activated).astype(jnp.bfloat16)
    grad_inputs = (
        jnp.einsum("scf,df->scd", grad_pre_gate, gate_mat, preferred_element_type=jnp.float32)
        + jnp.einsum("scf,df->scd", grad_pre_up, up_mat, preferred_element_type=jnp.float32)
    ).astype(jnp.bfloat16)
    grad_down = jnp.einsum("scf,scd->fd", hidden, cots, preferred_element_type=jnp.float32)
    grad_gate = jnp.einsum("scd,scf->df", inputs, grad_pre_gate, preferred_element_type=jnp.float32)
    grad_up = jnp.einsum("scd,scf->df", inputs, grad_pre_up, preferred_element_type=jnp.float32)
    return (jnp.concatenate([output, grad_inputs], axis=-1), grad_gate, grad_up, grad_down)


def attend_heads(query_rows, key_rows, value_rows):
    rows = query_rows.shape[0]
    devices = lax.psum(1, "blk")
    groups = devices // HEADS
    part = rows // groups
    kept = rows // 2
    scale = 1.0 / math.sqrt(HEAD)

    def by_head(block):
        return jnp.transpose(block.reshape(rows, HEADS, HEAD), (1, 0, 2))

    pairs = jnp.concatenate([by_head(key_rows), by_head(value_rows)], axis=-1)
    pairs = pairs.reshape(HEADS, 1, 2, kept, 2 * HEAD)
    pairs = jnp.broadcast_to(pairs, (HEADS, groups // 2, 2, kept, 2 * HEAD))
    pairs = pairs.reshape(devices, kept, 2 * HEAD)
    asked = jnp.transpose(query_rows.reshape(groups, part, HEADS, HEAD), (2, 0, 1, 3))
    asked = asked.reshape(devices, part, HEAD)
    asked = jnp.concatenate([asked, jnp.zeros_like(asked)], axis=-1)
    parcel = jnp.concatenate([pairs, asked], axis=1)
    got = lax.all_to_all(parcel, "blk", 0, 0, tiled=True)
    other = lax.ppermute(got[:, :kept, :], "blk", partner_pairs())
    steps = 4
    chunk = devices // steps

    def kernel(got_ref, other_ref, out_ref):
        step = pl.program_id(0)
        near = got_ref[:, :kept, :].reshape(devices * kept, 2 * HEAD)
        far = other_ref[...].reshape(devices * kept, 2 * HEAD)
        asked_now = got_ref[pl.ds(step * chunk, chunk), kept:, :].reshape(chunk * part, 2 * HEAD)
        dims = (((1,), (1,)), ((), ()))
        near_scores = lax.dot_general(asked_now, near, dims, preferred_element_type=jnp.float32) * scale
        far_scores = lax.dot_general(asked_now, far, dims, preferred_element_type=jnp.float32) * scale
        highest = jnp.maximum(
            jnp.max(near_scores, axis=-1, keepdims=True), jnp.max(far_scores, axis=-1, keepdims=True)
        )
        near_expo = jnp.exp(near_scores - highest)
        far_expo = jnp.exp(far_scores - highest)
        denom = jnp.sum(near_expo, axis=-1, keepdims=True) + jnp.sum(far_expo, axis=-1, keepdims=True)
        totals = jnp.dot(
            near_expo.astype(jnp.bfloat16), near, preferred_element_type=jnp.float32
        ) + jnp.dot(far_expo.astype(jnp.bfloat16), far, preferred_element_type=jnp.float32)
        out_ref[...] = (totals[:, HEAD:] / denom).astype(jnp.bfloat16).reshape(chunk, part, HEAD)

    queries_total = devices * part
    keys_total = devices * rows
    mixed = pl.pallas_call(
        kernel,
        grid=(steps,),
        in_specs=[
            pl.BlockSpec(got.shape, lambda i: (0, 0, 0)),
            pl.BlockSpec(other.shape, lambda i: (0, 0, 0)),
        ],
        out_specs=pl.BlockSpec((chunk, part, HEAD), lambda i: (i, 0, 0)),
        out_shape=jax.ShapeDtypeStruct((devices, part, HEAD), jnp.bfloat16),
        compiler_params=pltpu.CompilerParams(vmem_limit_bytes=48 * 1024 * 1024),
        cost_estimate=pl.CostEstimate(
            flops=4 * queries_total * keys_total * 2 * HEAD,
            transcendentals=queries_total * keys_total,
            bytes_accessed=(got.size + other.size) * 2 + queries_total * HEAD * 2,
        ),
    )(got, other)
    me = lax.axis_index("blk")
    order = (me + jnp.arange(devices)) % devices
    outgoing = mixed[order]
    arrived = [outgoing[0]] + [
        lax.ppermute(outgoing[k], "blk", [(b, (b + k) % devices) for b in range(devices)])
        for k in range(1, devices)
    ]
    back = jnp.stack(arrived)[(me - jnp.arange(devices)) % devices]
    back = jnp.transpose(back.reshape(HEADS, groups, part, HEAD), (1, 2, 0, 3))
    return back.reshape(rows, HEADS * HEAD)


def block(
    residual,
    queries,
    key_rows,
    value_rows,
    w_out,
    expert_ids,
    route_gates,
    cotangent,
    w_gate,
    w_up,
    w_down,
):
    row_count = queries.shape[1]
    route_experts = expert_ids[0].reshape(-1)
    gates = route_gates[0].reshape(-1)
    onehot = (route_experts[:, None] == jnp.arange(EXPERTS, dtype=jnp.int32)[None, :]).astype(
        jnp.int32
    )
    before = jnp.cumsum(onehot, axis=0) - onehot
    position = jnp.sum(before * onehot, axis=1)
    slot_index = route_experts * CAP + position
    grad_flat = cotangent[0].astype(jnp.float32)
    route_cots = (gates[:, None] * jnp.repeat(grad_flat, TOP, axis=0)).astype(jnp.bfloat16)
    half = CAP // PIECES
    slot_ids = jnp.arange(EXPERTS * CAP, dtype=jnp.int32).reshape(EXPERTS * PIECES, half)
    placing = (slot_ids[:, :, None] == slot_index[None, None, :]).astype(jnp.bfloat16)
    attended = attend_heads(queries[0], key_rows[0], value_rows[0])
    stream = residual[0].astype(jnp.float32) + jnp.dot(
        attended, w_out, preferred_element_type=jnp.float32
    )
    radius = jnp.sqrt(jnp.mean(stream * stream, axis=-1, keepdims=True) + 1e-06)
    unit = stream / radius
    normed = unit.astype(jnp.bfloat16)
    route_rows = jnp.concatenate([jnp.repeat(normed, TOP, axis=0), route_cots], axis=1)
    in_slots = jnp.einsum(
        "jcr,rw->jcw", placing, route_rows, preferred_element_type=jnp.float32
    ).astype(jnp.bfloat16)
    both_own, both_other = spread(in_slots)
    in_own, cot_own = both_own[..., :D], both_own[..., D:]
    in_other, cot_other = both_other[..., :D], both_other[..., D:]
    mats = (w_gate[0], w_up[0], w_down[0])
    own, gate_a, up_a, down_a = piece_pass(in_own, cot_own, *mats)
    other, gate_b, up_b, down_b = piece_pass(in_other, cot_other, *mats)
    theirs = lax.ppermute(other, "blk", partner_pairs())
    summed = (own.astype(jnp.float32) + theirs.astype(jnp.float32)).astype(jnp.bfloat16)
    back = to_anchor(summed)
    picking = (slot_index[:, None] == slot_ids.reshape(1, -1)).astype(jnp.bfloat16)
    picked = jnp.dot(
        picking, back.reshape(EXPERTS * CAP, 2 * D), preferred_element_type=jnp.float32
    )
    route_out = picked[:, :D]
    route_grad = picked[:, D:]
    grad_gate = (gate_a + gate_b).astype(jnp.bfloat16)[None]
    grad_up = (up_a + up_b).astype(jnp.bfloat16)[None]
    grad_down = (down_a + down_b).astype(jnp.bfloat16)[None]
    moe = jnp.sum((gates[:, None] * route_out).reshape(row_count, TOP, D), axis=1)
    block_out = (stream + moe).astype(jnp.bfloat16)[None]
    grad_unit = jnp.sum(route_grad.reshape(row_count, TOP, D), axis=1)
    grad_stream = (
        grad_flat + (grad_unit - unit * jnp.mean(grad_unit * unit, axis=-1, keepdims=True)) / radius
    )
    return (block_out, grad_stream.astype(jnp.bfloat16)[None], grad_gate, grad_up, grad_down)


def solution(mesh):
    return jax.shard_map(
        block,
        mesh=mesh,
        in_specs=(
            P("table", "blk", None),
            P("table", "blk", None),
            P("table", "blk", None),
            P("table", "blk", None),
            P(),
            P("table", "blk", None),
            P("table", "blk", None),
            P("table", "blk", None),
            P(("table", "blk"), None, None),
            P(("table", "blk"), None, None),
            P(("table", "blk"), None, None),
        ),
        out_specs=(
            P("table", "blk", None),
            P("table", "blk", None),
            P(("table", "blk"), None, None),
            P(("table", "blk"), None, None),
            P(("table", "blk"), None, None),
        ),
        check_vma=False,
    )
```

```python
import math

import jax
import jax.numpy as jnp
from jax import lax
from jax.experimental import pallas as pl
from jax.experimental.pallas import tpu as pltpu
from jax.sharding import PartitionSpec as P


D = 512
HEADS = 8
HEAD = 64
EXPERTS = 64
TOP = 2
PIECES = 2
CAP = 12


def silu_grad(pre):
    sig = jax.nn.sigmoid(pre)
    return sig * (1.0 + pre * (1.0 - sig))


def to_experts(buffer):
    return lax.all_to_all(buffer, ("table", "blk"), split_axis=0, concat_axis=0, tiled=True)


def to_anchor(buffer):
    return lax.all_to_all(buffer, ("table", "blk"), split_axis=0, concat_axis=0, tiled=True)


def partner_pairs():
    devices = lax.psum(1, "blk")
    return [(b, b ^ 1) for b in range(devices)]


def spread(slots):
    got = to_experts(slots)
    other = lax.ppermute(got, "blk", partner_pairs())
    return got, other


def piece_pass(inputs, cots, gate_mat, up_mat, down_mat):
    pre_gate = jnp.einsum("scd,df->scf", inputs, gate_mat, preferred_element_type=jnp.float32)
    pre_up = jnp.einsum("scd,df->scf", inputs, up_mat, preferred_element_type=jnp.float32)
    activated = jax.nn.silu(pre_gate)
    hidden = (activated * pre_up).astype(jnp.bfloat16)
    output = jnp.einsum(
        "scf,fd->scd", hidden, down_mat, preferred_element_type=jnp.float32
    ).astype(jnp.bfloat16)
    grad_hidden = jnp.einsum("scd,fd->scf", cots, down_mat, preferred_element_type=jnp.float32)
    grad_pre_gate = (grad_hidden * pre_up * silu_grad(pre_gate)).astype(jnp.bfloat16)
    grad_pre_up = (grad_hidden * activated).astype(jnp.bfloat16)
    grad_inputs = (
        jnp.einsum("scf,df->scd", grad_pre_gate, gate_mat, preferred_element_type=jnp.float32)
        + jnp.einsum("scf,df->scd", grad_pre_up, up_mat, preferred_element_type=jnp.float32)
    ).astype(jnp.bfloat16)
    grad_down = jnp.einsum("scf,scd->fd", hidden, cots, preferred_element_type=jnp.float32)
    grad_gate = jnp.einsum("scd,scf->df", inputs, grad_pre_gate, preferred_element_type=jnp.float32)
    grad_up = jnp.einsum("scd,scf->df", inputs, grad_pre_up, preferred_element_type=jnp.float32)
    return (jnp.concatenate([output, grad_inputs], axis=-1), grad_gate, grad_up, grad_down)


def attend_heads(query_rows, key_rows, value_rows):
    rows = query_rows.shape[0]
    devices = lax.psum(1, "blk")
    groups = devices // HEADS
    part = rows // groups
    kept = rows // 2
    scale = 1.0 / math.sqrt(HEAD)

    def pack(key_ref, value_ref, query_ref, parcel_ref):
        lane = lax.broadcasted_iota(jnp.int32, (rows, 2 * HEAD), 1)
        low = lane < HEAD
        for head in range(HEADS):
            cols = pl.ds((head // 2) * 2 * HEAD, 2 * HEAD)
            key_tile = key_ref[:, cols].astype(jnp.float32)
            value_tile = value_ref[:, cols].astype(jnp.float32)
            query_tile = query_ref[:, cols].astype(jnp.float32)
            if head % 2 == 0:
                both = jnp.where(low, key_tile, pltpu.roll(value_tile, HEAD, 1))
                ask = jnp.where(low, query_tile, 0.0)
            else:
                both = jnp.where(low, pltpu.roll(key_tile, HEAD, 1), value_tile)
                ask = jnp.where(low, pltpu.roll(query_tile, HEAD, 1), 0.0)
            both = both.astype(jnp.bfloat16)
            ask = ask.astype(jnp.bfloat16)
            for group in range(groups):
                dest = head * groups + group
                side = group % 2
                parcel_ref[dest, :kept, :] = both[side * kept : (side + 1) * kept]
                parcel_ref[dest, kept:, :] = ask[group * part : (group + 1) * part]

    parcel = pl.pallas_call(
        pack,
        out_shape=jax.ShapeDtypeStruct((devices, kept + part, 2 * HEAD), jnp.bfloat16),
    )(key_rows, value_rows, query_rows)
    got = lax.all_to_all(parcel, "blk", 0, 0, tiled=True)
    other = lax.ppermute(got, "blk", partner_pairs())
    steps = 2
    chunk = devices // steps

    def kernel(got_ref, other_ref, out_ref):
        step = pl.program_id(0)
        near = got_ref[:, :kept, :].reshape(devices * kept, 2 * HEAD)
        far = other_ref[:, :kept, :].reshape(devices * kept, 2 * HEAD)
        asked_now = got_ref[pl.ds(step * chunk, chunk), kept:, :].reshape(chunk * part, 2 * HEAD)
        dims = (((1,), (1,)), ((), ()))
        near_scores = lax.dot_general(asked_now, near, dims, preferred_element_type=jnp.float32) * scale
        far_scores = lax.dot_general(asked_now, far, dims, preferred_element_type=jnp.float32) * scale
        highest = jnp.maximum(
            jnp.max(near_scores, axis=-1, keepdims=True), jnp.max(far_scores, axis=-1, keepdims=True)
        )
        near_expo = jnp.exp(near_scores - highest)
        far_expo = jnp.exp(far_scores - highest)
        denom = jnp.sum(near_expo, axis=-1, keepdims=True) + jnp.sum(far_expo, axis=-1, keepdims=True)
        totals = jnp.dot(
            near_expo.astype(jnp.bfloat16), near, preferred_element_type=jnp.float32
        ) + jnp.dot(far_expo.astype(jnp.bfloat16), far, preferred_element_type=jnp.float32)
        out_ref[...] = (totals[:, HEAD:] / denom).astype(jnp.bfloat16).reshape(chunk, part, HEAD)

    queries_total = devices * part
    keys_total = devices * rows
    mixed = pl.pallas_call(
        kernel,
        grid=(steps,),
        in_specs=[
            pl.BlockSpec(got.shape, lambda i: (0, 0, 0)),
            pl.BlockSpec(other.shape, lambda i: (0, 0, 0)),
        ],
        out_specs=pl.BlockSpec((chunk, part, HEAD), lambda i: (i, 0, 0)),
        out_shape=jax.ShapeDtypeStruct((devices, part, HEAD), jnp.bfloat16),
        compiler_params=pltpu.CompilerParams(vmem_limit_bytes=48 * 1024 * 1024),
        cost_estimate=pl.CostEstimate(
            flops=4 * queries_total * keys_total * 2 * HEAD,
            transcendentals=queries_total * keys_total,
            bytes_accessed=(got.size + other.size) * 2 + queries_total * HEAD * 2,
        ),
    )(got, other)
    back = lax.all_to_all(mixed, "blk", 0, 0, tiled=True)
    back = jnp.transpose(back.reshape(HEADS, groups, part, HEAD), (1, 2, 0, 3))
    return back.reshape(rows, HEADS * HEAD)


def block(
    residual,
    queries,
    key_rows,
    value_rows,
    w_out,
    expert_ids,
    route_gates,
    cotangent,
    w_gate,
    w_up,
    w_down,
):
    row_count = queries.shape[1]
    route_experts = expert_ids[0].reshape(-1)
    gates = route_gates[0].reshape(-1)
    onehot = (route_experts[:, None] == jnp.arange(EXPERTS, dtype=jnp.int32)[None, :]).astype(
        jnp.int32
    )
    before = jnp.cumsum(onehot, axis=0) - onehot
    position = jnp.sum(before * onehot, axis=1)
    slot_index = route_experts * CAP + position
    grad_flat = cotangent[0].astype(jnp.float32)
    route_cots = (gates[:, None] * jnp.repeat(grad_flat, TOP, axis=0)).astype(jnp.bfloat16)
    half = CAP // PIECES
    slot_ids = jnp.arange(EXPERTS * CAP, dtype=jnp.int32).reshape(EXPERTS * PIECES, half)
    placing = (slot_ids[:, :, None] == slot_index[None, None, :]).astype(jnp.bfloat16)
    attended = attend_heads(queries[0], key_rows[0], value_rows[0])
    stream = residual[0].astype(jnp.float32) + jnp.dot(
        attended, w_out, preferred_element_type=jnp.float32
    )
    radius = jnp.sqrt(jnp.mean(stream * stream, axis=-1, keepdims=True) + 1e-06)
    unit = stream / radius
    normed = unit.astype(jnp.bfloat16)
    route_rows = jnp.concatenate([jnp.repeat(normed, TOP, axis=0), route_cots], axis=1)
    in_slots = jnp.einsum(
        "jcr,rw->jcw", placing, route_rows, preferred_element_type=jnp.float32
    ).astype(jnp.bfloat16)
    both_own, both_other = spread(in_slots)
    in_own, cot_own = both_own[..., :D], both_own[..., D:]
    in_other, cot_other = both_other[..., :D], both_other[..., D:]
    mats = (w_gate[0], w_up[0], w_down[0])
    own, gate_a, up_a, down_a = piece_pass(in_own, cot_own, *mats)
    other, gate_b, up_b, down_b = piece_pass(in_other, cot_other, *mats)
    theirs = lax.ppermute(other, "blk", partner_pairs())
    summed = (own.astype(jnp.float32) + theirs.astype(jnp.float32)).astype(jnp.bfloat16)
    back = to_anchor(summed)
    picking = (slot_index[:, None] == slot_ids.reshape(1, -1)).astype(jnp.bfloat16)
    picked = jnp.dot(
        picking, back.reshape(EXPERTS * CAP, 2 * D), preferred_element_type=jnp.float32
    )
    route_out = picked[:, :D]
    route_grad = picked[:, D:]
    grad_gate = (gate_a + gate_b).astype(jnp.bfloat16)[None]
    grad_up = (up_a + up_b).astype(jnp.bfloat16)[None]
    grad_down = (down_a + down_b).astype(jnp.bfloat16)[None]
    moe = jnp.sum((gates[:, None] * route_out).reshape(row_count, TOP, D), axis=1)
    block_out = (stream + moe).astype(jnp.bfloat16)[None]
    grad_unit = jnp.sum(route_grad.reshape(row_count, TOP, D), axis=1)
    grad_stream = (
        grad_flat + (grad_unit - unit * jnp.mean(grad_unit * unit, axis=-1, keepdims=True)) / radius
    )
    return (block_out, grad_stream.astype(jnp.bfloat16)[None], grad_gate, grad_up, grad_down)


def solution(mesh):
    return jax.shard_map(
        block,
        mesh=mesh,
        in_specs=(
            P("table", "blk", None),
            P("table", "blk", None),
            P("table", "blk", None),
            P("table", "blk", None),
            P(),
            P("table", "blk", None),
            P("table", "blk", None),
            P("table", "blk", None),
            P(("table", "blk"), None, None),
            P(("table", "blk"), None, None),
            P(("table", "blk"), None, None),
        ),
        out_specs=(
            P("table", "blk", None),
            P("table", "blk", None),
            P(("table", "blk"), None, None),
            P(("table", "blk"), None, None),
            P(("table", "blk"), None, None),
        ),
        check_vma=False,
    )
```

```python
import math

import jax
import jax.numpy as jnp
from jax import lax
from jax.experimental import pallas as pl
from jax.experimental.pallas import tpu as pltpu
from jax.sharding import PartitionSpec as P


D = 512
HEADS = 8
HEAD = 64
EXPERTS = 64
TOP = 2
PIECES = 2
CAP = 12


def silu_grad(pre):
    sig = jax.nn.sigmoid(pre)
    return sig * (1.0 + pre * (1.0 - sig))


def to_experts(buffer):
    return lax.all_to_all(buffer, ("table", "blk"), split_axis=0, concat_axis=0, tiled=True)


def to_anchor(buffer):
    return lax.all_to_all(buffer, ("table", "blk"), split_axis=0, concat_axis=0, tiled=True)


def partner_pairs():
    devices = lax.psum(1, "blk")
    return [(b, b ^ 1) for b in range(devices)]


def spread(slots):
    got = to_experts(slots)
    other = lax.ppermute(got, "blk", partner_pairs())
    return got, other


def piece_pass(inputs, cots, gate_mat, up_mat, down_mat):
    pre_gate = jnp.einsum("scd,df->scf", inputs, gate_mat, preferred_element_type=jnp.float32)
    pre_up = jnp.einsum("scd,df->scf", inputs, up_mat, preferred_element_type=jnp.float32)
    activated = jax.nn.silu(pre_gate)
    hidden = (activated * pre_up).astype(jnp.bfloat16)
    output = jnp.einsum(
        "scf,fd->scd", hidden, down_mat, preferred_element_type=jnp.float32
    ).astype(jnp.bfloat16)
    grad_hidden = jnp.einsum("scd,fd->scf", cots, down_mat, preferred_element_type=jnp.float32)
    grad_pre_gate = (grad_hidden * pre_up * silu_grad(pre_gate)).astype(jnp.bfloat16)
    grad_pre_up = (grad_hidden * activated).astype(jnp.bfloat16)
    grad_inputs = (
        jnp.einsum("scf,df->scd", grad_pre_gate, gate_mat, preferred_element_type=jnp.float32)
        + jnp.einsum("scf,df->scd", grad_pre_up, up_mat, preferred_element_type=jnp.float32)
    ).astype(jnp.bfloat16)
    grad_down = jnp.einsum("scf,scd->fd", hidden, cots, preferred_element_type=jnp.float32)
    grad_gate = jnp.einsum("scd,scf->df", inputs, grad_pre_gate, preferred_element_type=jnp.float32)
    grad_up = jnp.einsum("scd,scf->df", inputs, grad_pre_up, preferred_element_type=jnp.float32)
    return (jnp.concatenate([output, grad_inputs], axis=-1), grad_gate, grad_up, grad_down)


def attend_heads(query_rows, key_rows, value_rows):
    rows = query_rows.shape[0]
    devices = lax.psum(1, "blk")
    groups = devices // HEADS
    part = rows // groups
    kept = rows // 2
    scale = 1.0 / math.sqrt(HEAD)

    def pack(key_ref, value_ref, query_ref, parcel_ref):
        lane = lax.broadcasted_iota(jnp.int32, (rows, 2 * HEAD), 1)
        low = lane < HEAD
        for head in range(HEADS):
            cols = pl.ds((head // 2) * 2 * HEAD, 2 * HEAD)
            key_tile = key_ref[:, cols].astype(jnp.float32)
            value_tile = value_ref[:, cols].astype(jnp.float32)
            query_tile = query_ref[:, cols].astype(jnp.float32)
            if head % 2 == 0:
                both = jnp.where(low, key_tile, pltpu.roll(value_tile, HEAD, 1))
                ask = jnp.where(low, query_tile, 0.0)
            else:
                both = jnp.where(low, pltpu.roll(key_tile, HEAD, 1), value_tile)
                ask = jnp.where(low, pltpu.roll(query_tile, HEAD, 1), 0.0)
            both = both.astype(jnp.bfloat16)
            ask = ask.astype(jnp.bfloat16)
            for group in range(groups):
                dest = head * groups + group
                side = group % 2
                parcel_ref[dest, :kept, :] = both[side * kept : (side + 1) * kept]
                parcel_ref[dest, kept:, :] = ask[group * part : (group + 1) * part]

    parcel = pl.pallas_call(
        pack,
        out_shape=jax.ShapeDtypeStruct((devices, kept + part, 2 * HEAD), jnp.bfloat16),
    )(key_rows, value_rows, query_rows)
    got = lax.all_to_all(parcel, "blk", 0, 0, tiled=True)
    other = lax.ppermute(got[:, :kept, :], "blk", partner_pairs())
    steps = 8
    chunk = devices // steps

    def kernel(got_ref, other_ref, out_ref):
        step = pl.program_id(0)
        near = got_ref[:, :kept, :].reshape(devices * kept, 2 * HEAD)
        far = other_ref[...].reshape(devices * kept, 2 * HEAD)
        asked_now = got_ref[pl.ds(step * chunk, chunk), kept:, :].reshape(chunk * part, 2 * HEAD)
        dims = (((1,), (1,)), ((), ()))
        near_scores = lax.dot_general(asked_now, near, dims, preferred_element_type=jnp.float32) * scale
        far_scores = lax.dot_general(asked_now, far, dims, preferred_element_type=jnp.float32) * scale
        highest = jnp.maximum(
            jnp.max(near_scores, axis=-1, keepdims=True), jnp.max(far_scores, axis=-1, keepdims=True)
        )
        near_expo = jnp.exp(near_scores - highest)
        far_expo = jnp.exp(far_scores - highest)
        denom = jnp.sum(near_expo, axis=-1, keepdims=True) + jnp.sum(far_expo, axis=-1, keepdims=True)
        totals = jnp.dot(
            near_expo.astype(jnp.bfloat16), near, preferred_element_type=jnp.float32
        ) + jnp.dot(far_expo.astype(jnp.bfloat16), far, preferred_element_type=jnp.float32)
        out_ref[...] = (totals[:, HEAD:] / denom).astype(jnp.bfloat16).reshape(chunk, part, HEAD)

    queries_total = devices * part
    keys_total = devices * rows
    mixed = pl.pallas_call(
        kernel,
        grid=(steps,),
        in_specs=[
            pl.BlockSpec(got.shape, lambda i: (0, 0, 0)),
            pl.BlockSpec(other.shape, lambda i: (0, 0, 0)),
        ],
        out_specs=pl.BlockSpec((chunk, part, HEAD), lambda i: (i, 0, 0)),
        out_shape=jax.ShapeDtypeStruct((devices, part, HEAD), jnp.bfloat16),
        compiler_params=pltpu.CompilerParams(vmem_limit_bytes=48 * 1024 * 1024),
        cost_estimate=pl.CostEstimate(
            flops=4 * queries_total * keys_total * 2 * HEAD,
            transcendentals=queries_total * keys_total,
            bytes_accessed=(got.size + other.size) * 2 + queries_total * HEAD * 2,
        ),
    )(got, other)
    back = lax.all_to_all(mixed, "blk", 0, 0, tiled=True)
    back = jnp.transpose(back.reshape(HEADS, groups, part, HEAD), (1, 2, 0, 3))
    return back.reshape(rows, HEADS * HEAD)


def block(
    residual,
    queries,
    key_rows,
    value_rows,
    w_out,
    expert_ids,
    route_gates,
    cotangent,
    w_gate,
    w_up,
    w_down,
):
    row_count = queries.shape[1]
    route_experts = expert_ids[0].reshape(-1)
    gates = route_gates[0].reshape(-1)
    onehot = (route_experts[:, None] == jnp.arange(EXPERTS, dtype=jnp.int32)[None, :]).astype(
        jnp.int32
    )
    before = jnp.cumsum(onehot, axis=0) - onehot
    position = jnp.sum(before * onehot, axis=1)
    slot_index = route_experts * CAP + position
    grad_flat = cotangent[0].astype(jnp.float32)
    route_cots = (gates[:, None] * jnp.repeat(grad_flat, TOP, axis=0)).astype(jnp.bfloat16)
    half = CAP // PIECES
    slot_ids = jnp.arange(EXPERTS * CAP, dtype=jnp.int32).reshape(EXPERTS * PIECES, half)
    placing = (slot_ids[:, :, None] == slot_index[None, None, :]).astype(jnp.bfloat16)
    attended = attend_heads(queries[0], key_rows[0], value_rows[0])
    stream = residual[0].astype(jnp.float32) + jnp.dot(
        attended, w_out, preferred_element_type=jnp.float32
    )
    radius = jnp.sqrt(jnp.mean(stream * stream, axis=-1, keepdims=True) + 1e-06)
    unit = stream / radius
    normed = unit.astype(jnp.bfloat16)
    route_rows = jnp.concatenate([jnp.repeat(normed, TOP, axis=0), route_cots], axis=1)
    in_slots = jnp.einsum(
        "jcr,rw->jcw", placing, route_rows, preferred_element_type=jnp.float32
    ).astype(jnp.bfloat16)
    both_own, both_other = spread(in_slots)
    in_own, cot_own = both_own[..., :D], both_own[..., D:]
    in_other, cot_other = both_other[..., :D], both_other[..., D:]
    mats = (w_gate[0], w_up[0], w_down[0])
    own, gate_a, up_a, down_a = piece_pass(in_own, cot_own, *mats)
    other, gate_b, up_b, down_b = piece_pass(in_other, cot_other, *mats)
    theirs = lax.ppermute(other, "blk", partner_pairs())
    summed = (own.astype(jnp.float32) + theirs.astype(jnp.float32)).astype(jnp.bfloat16)
    back = to_anchor(summed)
    picking = (slot_index[:, None] == slot_ids.reshape(1, -1)).astype(jnp.bfloat16)
    picked = jnp.dot(
        picking, back.reshape(EXPERTS * CAP, 2 * D), preferred_element_type=jnp.float32
    )
    route_out = picked[:, :D]
    route_grad = picked[:, D:]
    grad_gate = (gate_a + gate_b).astype(jnp.bfloat16)[None]
    grad_up = (up_a + up_b).astype(jnp.bfloat16)[None]
    grad_down = (down_a + down_b).astype(jnp.bfloat16)[None]
    moe = jnp.sum((gates[:, None] * route_out).reshape(row_count, TOP, D), axis=1)
    block_out = (stream + moe).astype(jnp.bfloat16)[None]
    grad_unit = jnp.sum(route_grad.reshape(row_count, TOP, D), axis=1)
    grad_stream = (
        grad_flat + (grad_unit - unit * jnp.mean(grad_unit * unit, axis=-1, keepdims=True)) / radius
    )
    return (block_out, grad_stream.astype(jnp.bfloat16)[None], grad_gate, grad_up, grad_down)


def solution(mesh):
    return jax.shard_map(
        block,
        mesh=mesh,
        in_specs=(
            P("table", "blk", None),
            P("table", "blk", None),
            P("table", "blk", None),
            P("table", "blk", None),
            P(),
            P("table", "blk", None),
            P("table", "blk", None),
            P("table", "blk", None),
            P(("table", "blk"), None, None),
            P(("table", "blk"), None, None),
            P(("table", "blk"), None, None),
        ),
        out_specs=(
            P("table", "blk", None),
            P("table", "blk", None),
            P(("table", "blk"), None, None),
            P(("table", "blk"), None, None),
            P(("table", "blk"), None, None),
        ),
        check_vma=False,
    )
```

```python
import math

import jax
import jax.numpy as jnp
from jax import lax
from jax.experimental import pallas as pl
from jax.experimental.pallas import tpu as pltpu
from jax.sharding import PartitionSpec as P


D = 512
HEADS = 8
HEAD = 64
EXPERTS = 64
TOP = 2
PIECES = 2
CAP = 12


def silu_grad(pre):
    sig = jax.nn.sigmoid(pre)
    return sig * (1.0 + pre * (1.0 - sig))


def to_experts(buffer):
    return lax.all_to_all(buffer, ("table", "blk"), split_axis=0, concat_axis=0, tiled=True)


def to_anchor(buffer):
    return lax.all_to_all(buffer, ("table", "blk"), split_axis=0, concat_axis=0, tiled=True)


def partner_pairs():
    devices = lax.psum(1, "blk")
    return [(b, b ^ 1) for b in range(devices)]


def spread(slots):
    got = to_experts(slots)
    other = lax.ppermute(got, "blk", partner_pairs())
    return got, other


def piece_pass(inputs, cots, gate_mat, up_mat, down_mat):
    pre_gate = jnp.einsum("scd,df->scf", inputs, gate_mat, preferred_element_type=jnp.float32)
    pre_up = jnp.einsum("scd,df->scf", inputs, up_mat, preferred_element_type=jnp.float32)
    activated = jax.nn.silu(pre_gate)
    hidden = (activated * pre_up).astype(jnp.bfloat16)
    output = jnp.einsum(
        "scf,fd->scd", hidden, down_mat, preferred_element_type=jnp.float32
    ).astype(jnp.bfloat16)
    grad_hidden = jnp.einsum("scd,fd->scf", cots, down_mat, preferred_element_type=jnp.float32)
    grad_pre_gate = (grad_hidden * pre_up * silu_grad(pre_gate)).astype(jnp.bfloat16)
    grad_pre_up = (grad_hidden * activated).astype(jnp.bfloat16)
    grad_inputs = (
        jnp.einsum("scf,df->scd", grad_pre_gate, gate_mat, preferred_element_type=jnp.float32)
        + jnp.einsum("scf,df->scd", grad_pre_up, up_mat, preferred_element_type=jnp.float32)
    ).astype(jnp.bfloat16)
    grad_down = jnp.einsum("scf,scd->fd", hidden, cots, preferred_element_type=jnp.float32)
    grad_gate = jnp.einsum("scd,scf->df", inputs, grad_pre_gate, preferred_element_type=jnp.float32)
    grad_up = jnp.einsum("scd,scf->df", inputs, grad_pre_up, preferred_element_type=jnp.float32)
    return (jnp.concatenate([output, grad_inputs], axis=-1), grad_gate, grad_up, grad_down)


def attend_heads(query_rows, key_rows, value_rows):
    rows = query_rows.shape[0]
    devices = lax.psum(1, "blk")
    groups = devices // HEADS
    part = rows // groups
    kept = rows // 2
    scale = 1.0 / math.sqrt(HEAD)

    def pack(key_ref, value_ref, query_ref, parcel_ref):
        lane = lax.broadcasted_iota(jnp.int32, (rows, 2 * HEAD), 1)
        low = lane < HEAD
        for head in range(HEADS):
            cols = pl.ds((head // 2) * 2 * HEAD, 2 * HEAD)
            key_tile = key_ref[:, cols]
            value_tile = value_ref[:, cols]
            query_tile = query_ref[:, cols].astype(jnp.float32)
            if head % 2 == 0:
                both = jnp.where(low, key_tile, pltpu.roll(value_tile, HEAD, 1))
                ask = jnp.where(low, query_tile * scale, 0.0)
            else:
                both = jnp.where(low, pltpu.roll(key_tile, HEAD, 1), value_tile)
                ask = jnp.where(low, pltpu.roll(query_tile * scale, HEAD, 1), 0.0)
            both = both.astype(jnp.bfloat16)
            ask = ask.astype(jnp.bfloat16)
            for group in range(groups):
                dest = head * groups + group
                side = group % 2
                parcel_ref[dest, :kept, :] = both[side * kept : (side + 1) * kept]
                parcel_ref[dest, kept:, :] = ask[group * part : (group + 1) * part]

    parcel = pl.pallas_call(
        pack,
        out_shape=jax.ShapeDtypeStruct((devices, kept + part, 2 * HEAD), jnp.bfloat16),
    )(key_rows, value_rows, query_rows)
    got = lax.all_to_all(parcel, "blk", 0, 0, tiled=True)
    other = lax.ppermute(got[:, :kept, :], "blk", partner_pairs())
    steps = 4
    chunk = devices // steps

    def kernel(got_ref, other_ref, out_ref):
        step = pl.program_id(0)
        near = got_ref[:, :kept, :].reshape(devices * kept, 2 * HEAD)
        far = other_ref[...].reshape(devices * kept, 2 * HEAD)
        asked_now = got_ref[pl.ds(step * chunk, chunk), kept:, :].reshape(chunk * part, 2 * HEAD)
        dims = (((1,), (1,)), ((), ()))
        near_scores = lax.dot_general(asked_now, near, dims, preferred_element_type=jnp.float32)
        far_scores = lax.dot_general(asked_now, far, dims, preferred_element_type=jnp.float32)
        highest = jnp.maximum(
            jnp.max(near_scores, axis=-1, keepdims=True), jnp.max(far_scores, axis=-1, keepdims=True)
        )
        near_expo = jnp.exp(near_scores - highest)
        far_expo = jnp.exp(far_scores - highest)
        denom = jnp.sum(near_expo, axis=-1, keepdims=True) + jnp.sum(far_expo, axis=-1, keepdims=True)
        totals = jnp.dot(
            near_expo.astype(jnp.bfloat16), near, preferred_element_type=jnp.float32
        ) + jnp.dot(far_expo.astype(jnp.bfloat16), far, preferred_element_type=jnp.float32)
        out_ref[...] = (totals[:, HEAD:] / denom).astype(jnp.bfloat16).reshape(chunk, part, HEAD)

    queries_total = devices * part
    keys_total = devices * rows
    mixed = pl.pallas_call(
        kernel,
        grid=(steps,),
        in_specs=[
            pl.BlockSpec(got.shape, lambda i: (0, 0, 0)),
            pl.BlockSpec(other.shape, lambda i: (0, 0, 0)),
        ],
        out_specs=pl.BlockSpec((chunk, part, HEAD), lambda i: (i, 0, 0)),
        out_shape=jax.ShapeDtypeStruct((devices, part, HEAD), jnp.bfloat16),
        compiler_params=pltpu.CompilerParams(vmem_limit_bytes=48 * 1024 * 1024),
        cost_estimate=pl.CostEstimate(
            flops=4 * queries_total * keys_total * 2 * HEAD,
            transcendentals=queries_total * keys_total,
            bytes_accessed=(got.size + other.size) * 2 + queries_total * HEAD * 2,
        ),
    )(got, other)
    back = lax.all_to_all(mixed, "blk", 0, 0, tiled=True)
    back = jnp.transpose(back.reshape(HEADS, groups, part, HEAD), (1, 2, 0, 3))
    return back.reshape(rows, HEADS * HEAD)


def block(
    residual,
    queries,
    key_rows,
    value_rows,
    w_out,
    expert_ids,
    route_gates,
    cotangent,
    w_gate,
    w_up,
    w_down,
):
    row_count = queries.shape[1]
    route_experts = expert_ids[0].reshape(-1)
    gates = route_gates[0].reshape(-1)
    onehot = (route_experts[:, None] == jnp.arange(EXPERTS, dtype=jnp.int32)[None, :]).astype(
        jnp.int32
    )
    before = jnp.cumsum(onehot, axis=0) - onehot
    position = jnp.sum(before * onehot, axis=1)
    slot_index = route_experts * CAP + position
    grad_flat = cotangent[0].astype(jnp.float32)
    route_cots = (gates[:, None] * jnp.repeat(grad_flat, TOP, axis=0)).astype(jnp.bfloat16)
    half = CAP // PIECES
    slot_ids = jnp.arange(EXPERTS * CAP, dtype=jnp.int32).reshape(EXPERTS * PIECES, half)
    placing = (slot_ids[:, :, None] == slot_index[None, None, :]).astype(jnp.bfloat16)
    attended = attend_heads(queries[0], key_rows[0], value_rows[0])
    stream = residual[0].astype(jnp.float32) + jnp.dot(
        attended, w_out, preferred_element_type=jnp.float32
    )
    radius = jnp.sqrt(jnp.mean(stream * stream, axis=-1, keepdims=True) + 1e-06)
    unit = stream / radius
    normed = unit.astype(jnp.bfloat16)
    route_rows = jnp.concatenate([jnp.repeat(normed, TOP, axis=0), route_cots], axis=1)
    in_slots = jnp.einsum(
        "jcr,rw->jcw", placing, route_rows, preferred_element_type=jnp.float32
    ).astype(jnp.bfloat16)
    both_own, both_other = spread(in_slots)
    in_own, cot_own = both_own[..., :D], both_own[..., D:]
    in_other, cot_other = both_other[..., :D], both_other[..., D:]
    mats = (w_gate[0], w_up[0], w_down[0])
    own, gate_a, up_a, down_a = piece_pass(in_own, cot_own, *mats)
    other, gate_b, up_b, down_b = piece_pass(in_other, cot_other, *mats)
    theirs = lax.ppermute(other, "blk", partner_pairs())
    summed = (own.astype(jnp.float32) + theirs.astype(jnp.float32)).astype(jnp.bfloat16)
    back = to_anchor(summed)
    picking = (slot_index[:, None] == slot_ids.reshape(1, -1)).astype(jnp.bfloat16)
    picked = jnp.dot(
        picking, back.reshape(EXPERTS * CAP, 2 * D), preferred_element_type=jnp.float32
    )
    route_out = picked[:, :D]
    route_grad = picked[:, D:]
    grad_gate = (gate_a + gate_b).astype(jnp.bfloat16)[None]
    grad_up = (up_a + up_b).astype(jnp.bfloat16)[None]
    grad_down = (down_a + down_b).astype(jnp.bfloat16)[None]
    moe = jnp.sum((gates[:, None] * route_out).reshape(row_count, TOP, D), axis=1)
    block_out = (stream + moe).astype(jnp.bfloat16)[None]
    grad_unit = jnp.sum(route_grad.reshape(row_count, TOP, D), axis=1)
    grad_stream = (
        grad_flat + (grad_unit - unit * jnp.mean(grad_unit * unit, axis=-1, keepdims=True)) / radius
    )
    return (block_out, grad_stream.astype(jnp.bfloat16)[None], grad_gate, grad_up, grad_down)


def solution(mesh):
    return jax.shard_map(
        block,
        mesh=mesh,
        in_specs=(
            P("table", "blk", None),
            P("table", "blk", None),
            P("table", "blk", None),
            P("table", "blk", None),
            P(),
            P("table", "blk", None),
            P("table", "blk", None),
            P("table", "blk", None),
            P(("table", "blk"), None, None),
            P(("table", "blk"), None, None),
            P(("table", "blk"), None, None),
        ),
        out_specs=(
            P("table", "blk", None),
            P("table", "blk", None),
            P(("table", "blk"), None, None),
            P(("table", "blk"), None, None),
            P(("table", "blk"), None, None),
        ),
        check_vma=False,
    )
```
